256 devices in a mesh: expert: 32 (over z, y_hi, core), dp: 8 (over x, y_lo).
Axes of the slice: x: 4, y: 4 (y_hi: 2, y_lo: 2; y = y_hi * 2 + y_lo), z: 8, core: 2. Of those that a mesh axis runs over, the one named last changes fastest.
Arguments:
- tokens: bfloat16 [32768, 2048], P(('expert', 'dp')), may hold values from -6 to 6
- targets: bfloat16 [32768, 2048], P(('expert', 'dp')), may hold values from -6 to 6
- router: bfloat16 [2048, 32], replicated, may hold values from -0.125 to 0.125
- picks: int32 [32768, 32, 4], P(('expert', 'dp')), may hold values from 0 to 1, as said below
- w_gate_up: bfloat16 [32, 2, 1408, 2048], P('expert', None, 'dp'), may hold values from -0.125 to 0.125
- w_down: bfloat16 [32, 1408, 2048], P('expert', 'dp'), may hold values from -0.15625 to 0.15625
- v_gate_up: bfloat16 [32, 2, 1408, 2048], P('expert', None, 'dp'), may hold values from -0.125 to 0.125
- v_down: bfloat16 [32, 1408, 2048], P('expert', 'dp'), may hold values from -0.15625 to 0.15625
Outputs:
- mixed: bfloat16 [32768, 2048], P(('expert', 'dp'))
- hvp_gate_up: float32 [32, 2, 1408, 2048], P('expert', None, 'dp')
- hvp_down: float32 [32, 1408, 2048], P('expert', 'dp')
The draws below stay inside these ranges and needn't reach their ends.
Inputs may be any that keep to these rules, and one draw needn't show every extreme that they name: In every block of 128 tokens (one device's rows), for each expert e and slot c exactly one token t has picks[t, e, c] = 1, and an expert never picks a token twice.
All inputs are finite; a program needn't handle non-finite values.
Results may differ from the reference program's by a relative error of at most 0.009.
Values may be sent and summed in bfloat16 or wider, within the bound.
No kernel may reach another device: no remote copies, remote signals or barrier semaphores. Data moves between devices by JAX's collectives and lax.ppermute only.
A program may use at most 128 MiB of HBM per device.

```python
import math
import jax
import jax.numpy as jnp
from jax import lax

D = 2048
FF = 1408
TOK_DEV = 128
CAP = 4
EXPERTS = 32
TOKENS = 32768


def draw_picks(key, part):
    blocks = TOKENS // TOK_DEV
    raw = jax.random.randint(key, (blocks, EXPERTS, TOK_DEV), 0, 1 << 20)
    scores = raw * TOK_DEV + jnp.arange(TOK_DEV, dtype=jnp.int32)
    order = jnp.argsort(scores, axis=-1)
    chosen = order[:, :, :CAP]
    hits = (jnp.arange(TOK_DEV, dtype=jnp.int32)[None, :, None, None] == chosen[:, None, :, :]).astype(jnp.int32)
    return hits.reshape(TOKENS, EXPERTS, CAP)


def level_of(rng, dims, cuts, low, top_value):
    level = 1.0
    for axis_at, shards_of in cuts:
        draws = jax.random.uniform(jax.random.fold_in(jax.random.fold_in(rng, 6), axis_at), (shards_of,), jnp.float32, low / len(cuts), top_value / len(cuts))
        level = level * jnp.repeat(jnp.exp(draws), dims[axis_at] // shards_of).reshape((-1,) + (1,) * (len(dims) - 1 - axis_at))
    return level


def normal_values(own_key, shape, deviation, reach, cuts=(), kind=jnp.bfloat16):
    factor_of = level_of(own_key, shape, cuts, -0.22, 0.18) if cuts else 1.0
    array = jax.random.normal(own_key, shape, jnp.float32) * deviation * factor_of
    return jnp.minimum(jnp.maximum(array, -reach), reach).astype(kind)


def setup_inputs(seed: int = 0) -> dict:
    key_list = jax.random.split(jax.random.key(seed), 9)
    tokens = normal_values(key_list[0], (TOKENS, D), 1.0, 6.0, ((0, 256),))
    targets = normal_values(key_list[1], (TOKENS, D), 1.0, 6.0, ((0, 256),))
    router = normal_values(key_list[2], (D, EXPERTS), D ** -0.5, 0.125)
    picks = draw_picks(jax.random.fold_in(key_list[8], 71), 0)
    w_gate_up = normal_values(key_list[4], (EXPERTS, 2, FF, D), D ** -0.5, 0.125, ((0, 32), (2, 8)))
    w_down = normal_values(key_list[5], (EXPERTS, FF, D), FF ** -0.5, 0.15625, ((0, 32), (1, 8)))
    v_gate_up = normal_values(key_list[6], (EXPERTS, 2, FF, D), D ** -0.5, 0.125, ((0, 32), (2, 8)))
    v_down = normal_values(key_list[7], (EXPERTS, FF, D), FF ** -0.5, 0.15625, ((0, 32), (1, 8)))
    return dict(tokens=tokens, targets=targets, router=router, picks=picks, w_gate_up=w_gate_up, w_down=w_down, v_gate_up=v_gate_up, v_down=v_down)


def forward_pieces(rows, wgu, vgu):
    gate_pre = jnp.dot(rows, wgu[0].T, preferred_element_type=jnp.float32)
    up_pre = jnp.dot(rows, wgu[1].T, preferred_element_type=jnp.float32)
    gate_dot = jnp.dot(rows, vgu[0].T, preferred_element_type=jnp.float32)
    up_dot = jnp.dot(rows, vgu[1].T, preferred_element_type=jnp.float32)
    sigma = jax.nn.sigmoid(gate_pre)
    active = gate_pre * sigma
    slope = sigma * (1.0 + gate_pre * (1.0 - sigma))
    curve = sigma * (1.0 - sigma) * (2.0 + gate_pre * (1.0 - 2.0 * sigma))
    act_dot = slope * gate_dot
    hidden = (active * up_pre).astype(jnp.bfloat16)
    hidden_dot = (act_dot * up_pre + active * up_dot).astype(jnp.bfloat16)
    return (up_pre, gate_dot, up_dot, active, slope, curve, act_dot, hidden, hidden_dot)

def reference(tokens, targets, router, picks, w_gate_up, w_down, v_gate_up, v_down):
    blocks = TOKENS // TOK_DEV
    gates = jax.nn.sigmoid(jnp.dot(tokens, router, preferred_element_type=jnp.float32))
    offsets = jnp.arange(TOK_DEV, dtype=jnp.int32)
    where = lax.optimization_barrier(jnp.sum(picks.reshape(blocks, TOK_DEV, EXPERTS, CAP) * offsets[None, :, None, None], axis=1))
    index = where + (jnp.arange(blocks, dtype=jnp.int32) * TOK_DEV)[:, None, None]
    index = jnp.transpose(index, (1, 0, 2)).reshape(EXPERTS, blocks * CAP).astype(jnp.int32)
    picked = jnp.take_along_axis(gates.T, index, axis=1)
    scale = 1.0 / math.sqrt(blocks * CAP)

    def forward(item):
        wgu, wdown, vgu, vdown, rows_index = item
        rows = tokens[rows_index]
        pieces = forward_pieces(rows, wgu, vgu)
        hidden, hidden_dot = (pieces[7], pieces[8])
        result = jnp.dot(hidden, wdown, preferred_element_type=jnp.float32)
        result_dot = jnp.dot(hidden_dot, wdown, preferred_element_type=jnp.float32) + jnp.dot(hidden, vdown, preferred_element_type=jnp.float32)
        return (result.astype(jnp.bfloat16), result_dot.astype(jnp.bfloat16))
    outs, outs_dot = lax.map(forward, (w_gate_up, w_down, v_gate_up, v_down, index))
    flat = index.reshape(-1)
    weight = picked.reshape(-1, 1)
    combined = jnp.zeros((TOKENS, D), jnp.float32).at[flat].add(weight * outs.reshape(-1, D).astype(jnp.float32))
    combined_dot = jnp.zeros((TOKENS, D), jnp.float32).at[flat].add(weight * outs_dot.reshape(-1, D).astype(jnp.float32))
    mixed = combined.astype(jnp.bfloat16)
    resid = scale * (combined - targets.astype(jnp.float32))
    resid_dot = scale * combined_dot

    def backward(item):
        wgu, wdown, vgu, vdown, rows_index, gate_col = item
        rows = tokens[rows_index]
        up_pre, gate_dot, up_dot, active, slope, curve, act_dot, hidden, hidden_dot = forward_pieces(rows, wgu, vgu)
        cot = (gate_col[:, None] * resid[rows_index]).astype(jnp.bfloat16)
        cot_dot = (gate_col[:, None] * resid_dot[rows_index]).astype(jnp.bfloat16)
        grad_hid = jnp.dot(cot, wdown.T, preferred_element_type=jnp.float32)
        grad_hdot = jnp.dot(cot_dot, wdown.T, preferred_element_type=jnp.float32) + jnp.dot(cot, vdown.T, preferred_element_type=jnp.float32)
        down_term = jnp.dot(hidden_dot.T, cot, preferred_element_type=jnp.float32) + jnp.dot(hidden.T, cot_dot, preferred_element_type=jnp.float32)
        gate_term = ((grad_hdot * up_pre + grad_hid * up_dot) * slope + grad_hid * up_pre * curve * gate_dot).astype(jnp.bfloat16)
        up_term = (grad_hdot * active + grad_hid * act_dot).astype(jnp.bfloat16)
        hvp_gate = jnp.dot(gate_term.T, rows, preferred_element_type=jnp.float32)
        hvp_up = jnp.dot(up_term.T, rows, preferred_element_type=jnp.float32)
        return (jnp.stack([hvp_gate, hvp_up]), down_term)
    hvp_gate_up, hvp_down = lax.map(backward, (w_gate_up, w_down, v_gate_up, v_down, index, picked))
    return (mixed, hvp_gate_up, hvp_down)
```

```python
import math

import jax
import jax.numpy as jnp
from jax import lax
from jax.sharding import PartitionSpec as P


def regroup(block, lead):
    count, total, width = block.shape
    parted = block.reshape(count, lead, total // lead, width)
    return jnp.swapaxes(parted, 0, 1).reshape(lead, count * total // lead, width)


def gather_dp(block):
    n_dp = lax.axis_size("dp")
    copies = jnp.broadcast_to(block[None], (n_dp,) + block.shape)
    got = lax.all_to_all(copies, "dp", split_axis=0, concat_axis=0, tiled=True)
    k, e, r, d = block.shape
    return jnp.moveaxis(got, 0, 2).reshape(k, e, n_dp * r, d)


def scatter_sum_dp(part):
    n_dp = lax.axis_size("dp")
    k, e, rows, d = part.shape
    blocks = jnp.moveaxis(part.reshape(k, e, n_dp, rows // n_dp, d), 2, 0)
    got = lax.all_to_all(blocks, "dp", split_axis=0, concat_axis=0, tiled=True)
    return jnp.sum(got.astype(jnp.float32), axis=0)


def local(tokens, targets, router, picks, w_gate_up, w_down, v_gate_up, v_down):
    highest = lax.Precision.HIGHEST
    n_exp = lax.axis_size("expert")
    exp_dev = w_down.shape[0]
    onehot = picks.astype(jnp.bfloat16)
    gates = jax.nn.sigmoid(jnp.dot(tokens, router, preferred_element_type=jnp.float32))
    outgoing = jnp.einsum("tec,td->ecd", onehot, tokens, preferred_element_type=jnp.float32).astype(
        jnp.bfloat16
    )
    arrived = lax.all_to_all(outgoing, "expert", split_axis=0, concat_axis=0, tiled=True)
    rows = gather_dp(regroup(arrived, exp_dev)[None])[0]
    scale = 1.0 / math.sqrt(rows.shape[1])
    primal = jnp.einsum("ekfd,erd->ekfr", w_gate_up, rows, preferred_element_type=jnp.float32)
    tangent = jnp.einsum("ekfd,erd->ekfr", v_gate_up, rows, preferred_element_type=jnp.float32)
    gate_pre, up_pre = (primal[:, 0], primal[:, 1])
    gate_dot, up_dot = (tangent[:, 0], tangent[:, 1])
    sigma = jax.nn.sigmoid(gate_pre)
    active = gate_pre * sigma
    slope = sigma * (1.0 + gate_pre * (1.0 - sigma))
    curve = sigma * (1.0 - sigma) * (2.0 + gate_pre * (1.0 - 2.0 * sigma))
    act_dot = slope * gate_dot
    hidden = (active * up_pre).astype(jnp.bfloat16)
    hidden_dot = (act_dot * up_pre + active * up_dot).astype(jnp.bfloat16)
    part_out = jnp.einsum("efr,efd->erd", hidden, w_down, preferred_element_type=jnp.float32)
    part_dot = jnp.einsum(
        "efr,efd->erd", hidden_dot, w_down, preferred_element_type=jnp.float32
    ) + jnp.einsum("efr,efd->erd", hidden, v_down, preferred_element_type=jnp.float32)
    own_both = scatter_sum_dp(jnp.stack([part_out, part_dot]).astype(jnp.bfloat16))
    back_both = jnp.stack(
        [regroup(own_both[0].astype(jnp.bfloat16), n_exp), regroup(own_both[1].astype(jnp.bfloat16), n_exp)],
        axis=1,
    )
    ret_both = lax.all_to_all(back_both, "expert", split_axis=0, concat_axis=0, tiled=True)
    ret_out, ret_dot = (ret_both[:, 0], ret_both[:, 1])
    ret_out = ret_out.astype(jnp.float32)
    ret_dot = ret_dot.astype(jnp.float32)
    weighted = picks.astype(jnp.float32) * gates[:, :, None]
    combined = jnp.einsum("tec,ecd->td", weighted, ret_out, precision=highest)
    combined_dot = jnp.einsum("tec,ecd->td", weighted, ret_dot, precision=highest)
    mixed = combined.astype(jnp.bfloat16)
    resid = scale * (combined - targets.astype(jnp.float32))
    resid_dot = scale * combined_dot
    cot_send = jnp.einsum("tec,td->ecd", weighted, resid, precision=highest).astype(jnp.bfloat16)
    cdot_send = jnp.einsum("tec,td->ecd", weighted, resid_dot, precision=highest).astype(
        jnp.bfloat16
    )
    both_got = lax.all_to_all(
        jnp.stack([cot_send, cdot_send], axis=1), "expert", split_axis=0, concat_axis=0, tiled=True
    )
    own_both = jnp.stack([regroup(both_got[:, 0], exp_dev), regroup(both_got[:, 1], exp_dev)])
    both_rows = gather_dp(own_both)
    cot_rows, cdot_rows = (both_rows[0], both_rows[1])
    grad_hid = jnp.einsum("erd,efd->efr", cot_rows, w_down, preferred_element_type=jnp.float32)
    grad_hdot = jnp.einsum(
        "erd,efd->efr", cdot_rows, w_down, preferred_element_type=jnp.float32
    ) + jnp.einsum("erd,efd->efr", cot_rows, v_down, preferred_element_type=jnp.float32)
    hvp_down = jnp.einsum(
        "efr,erd->efd", hidden_dot, cot_rows, preferred_element_type=jnp.float32
    ) + jnp.einsum("efr,erd->efd", hidden, cdot_rows, preferred_element_type=jnp.float32)
    gate_term = (
        (grad_hdot * up_pre + grad_hid * up_dot) * slope + grad_hid * up_pre * curve * gate_dot
    ).astype(jnp.bfloat16)
    up_term = (grad_hdot * active + grad_hid * act_dot).astype(jnp.bfloat16)
    both_terms = jnp.stack([gate_term, up_term], axis=1)
    hvp_gate_up = jnp.einsum("ekfr,erd->ekfd", both_terms, rows, preferred_element_type=jnp.float32)
    return (mixed, hvp_gate_up, hvp_down)


def solution(mesh):
    placed = (
        P(("expert", "dp"), None),
        P(("expert", "dp"), None),
        P(),
        P(("expert", "dp"), None, None),
        P("expert", None, "dp", None),
        P("expert", "dp", None),
        P("expert", None, "dp", None),
        P("expert", "dp", None),
    )
    return jax.shard_map(
        local,
        mesh=mesh,
        in_specs=placed,
        out_specs=(
            P(("expert", "dp"), None),
            P("expert", None, "dp", None),
            P("expert", "dp", None),
        ),
        check_vma=False,
    )
```

```python
import math

import jax
import jax.numpy as jnp
from jax import lax
from jax.sharding import PartitionSpec as P


def regroup(block, lead):
    count, total, width = block.shape
    parted = block.reshape(count, lead, total // lead, width)
    return jnp.swapaxes(parted, 0, 1).reshape(lead, count * total // lead, width)


def _perms(n_dp):
    nx = n_dp // 2
    idx = lambda a, b: 2 * (a % nx) + b
    partner = [(idx(a, b), idx(a, 1 - b)) for a in range(nx) for b in range(2)]
    xplus = [(idx(a, b), idx(a + 1, b)) for a in range(nx) for b in range(2)]
    xminus = [(idx(a, b), idx(a - 1, b)) for a in range(nx) for b in range(2)]
    return partner, xplus, xminus


def tree_gather(block):
    partner, xplus, xminus = _perms(lax.axis_size("dp"))
    send = lambda v, perm: lax.ppermute(v, "dp", perm)
    half = block.shape[0] // 2
    Pb = send(block, partner)
    L = send(block, xplus)
    R = send(block, xminus)
    O = jnp.concatenate([send(L[:half], xplus), send(R[half:], xminus)])
    PL = send(Pb, xplus)
    PR = send(Pb, xminus)
    Q = send(O, partner)
    return jnp.stack([block, Pb, L, R, O, PL, PR, Q])


def tree_scatter_sum(acc):
    partner, xplus, xminus = _perms(lax.axis_size("dp"))
    send = lambda v, perm: lax.ppermute(v.astype(jnp.bfloat16), "dp", perm).astype(jnp.float32)
    half = acc.shape[1] // 2
    a4 = acc[4] + send(acc[7], partner)
    a2 = acc[2] + jnp.concatenate([send(a4[:half], xminus), jnp.zeros_like(a4[half:])])
    a3 = acc[3] + jnp.concatenate([jnp.zeros_like(a4[:half]), send(a4[half:], xplus)])
    a1 = acc[1] + send(acc[5], xminus) + send(acc[6], xplus)
    return acc[0] + send(a1, partner) + send(a2, xminus) + send(a3, xplus)


def gather_dp(block):
    k, e, r, d = block.shape
    got = tree_gather(jnp.moveaxis(block, 2, 0))
    return jnp.moveaxis(got.reshape(-1, k, e, d), 0, 2)


def scatter_sum_dp(part):
    n_dp = lax.axis_size("dp")
    k, e, rows, d = part.shape
    blocks = jnp.moveaxis(part.astype(jnp.float32).reshape(k, e, n_dp, rows // n_dp, d), 2, 0)
    return tree_scatter_sum(blocks)


def local(tokens, targets, router, picks, w_gate_up, w_down, v_gate_up, v_down):
    highest = lax.Precision.HIGHEST
    n_exp = lax.axis_size("expert")
    exp_dev = w_down.shape[0]
    onehot = picks.astype(jnp.bfloat16)
    gates = jax.nn.sigmoid(jnp.dot(tokens, router, preferred_element_type=jnp.float32))
    outgoing = jnp.einsum("tec,td->ecd", onehot, tokens, preferred_element_type=jnp.float32).astype(
        jnp.bfloat16
    )
    arrived = lax.all_to_all(outgoing, "expert", split_axis=0, concat_axis=0, tiled=True)
    rows = gather_dp(regroup(arrived, exp_dev)[None])[0]
    scale = 1.0 / math.sqrt(rows.shape[1])
    primal = jnp.einsum("ekfd,erd->ekfr", w_gate_up, rows, preferred_element_type=jnp.float32)
    tangent = jnp.einsum("ekfd,erd->ekfr", v_gate_up, rows, preferred_element_type=jnp.float32)
    gate_pre, up_pre = (primal[:, 0], primal[:, 1])
    gate_dot, up_dot = (tangent[:, 0], tangent[:, 1])
    sigma = jax.nn.sigmoid(gate_pre)
    active = gate_pre * sigma
    slope = sigma * (1.0 + gate_pre * (1.0 - sigma))
    curve = sigma * (1.0 - sigma) * (2.0 + gate_pre * (1.0 - 2.0 * sigma))
    act_dot = slope * gate_dot
    hidden = (active * up_pre).astype(jnp.bfloat16)
    hidden_dot = (act_dot * up_pre + active * up_dot).astype(jnp.bfloat16)
    part_out = jnp.einsum("efr,efd->erd", hidden, w_down, preferred_element_type=jnp.float32)
    part_dot = jnp.einsum(
        "efr,efd->erd", hidden_dot, w_down, preferred_element_type=jnp.float32
    ) + jnp.einsum("efr,efd->erd", hidden, v_down, preferred_element_type=jnp.float32)
    own_both = scatter_sum_dp(jnp.stack([part_out, part_dot]))
    back_both = jnp.stack(
        [regroup(own_both[0].astype(jnp.bfloat16), n_exp), regroup(own_both[1].astype(jnp.bfloat16), n_exp)],
        axis=1,
    )
    ret_both = lax.all_to_all(back_both, "expert", split_axis=0, concat_axis=0, tiled=True)
    ret_out, ret_dot = (ret_both[:, 0], ret_both[:, 1])
    ret_out = ret_out.astype(jnp.float32)
    ret_dot = ret_dot.astype(jnp.float32)
    weighted = picks.astype(jnp.float32) * gates[:, :, None]
    combined = jnp.einsum("tec,ecd->td", weighted, ret_out, precision=highest)
    combined_dot = jnp.einsum("tec,ecd->td", weighted, ret_dot, precision=highest)
    mixed = combined.astype(jnp.bfloat16)
    resid = scale * (combined - targets.astype(jnp.float32))
    resid_dot = scale * combined_dot
    cot_send = jnp.einsum("tec,td->ecd", weighted, resid, precision=highest).astype(jnp.bfloat16)
    cdot_send = jnp.einsum("tec,td->ecd", weighted, resid_dot, precision=highest).astype(
        jnp.bfloat16
    )
    both_got = lax.all_to_all(
        jnp.stack([cot_send, cdot_send], axis=1), "expert", split_axis=0, concat_axis=0, tiled=True
    )
    own_both = jnp.stack([regroup(both_got[:, 0], exp_dev), regroup(both_got[:, 1], exp_dev)])
    both_rows = gather_dp(own_both)
    cot_rows, cdot_rows = (both_rows[0], both_rows[1])
    grad_hid = jnp.einsum("erd,efd->efr", cot_rows, w_down, preferred_element_type=jnp.float32)
    grad_hdot = jnp.einsum(
        "erd,efd->efr", cdot_rows, w_down, preferred_element_type=jnp.float32
    ) + jnp.einsum("erd,efd->efr", cot_rows, v_down, preferred_element_type=jnp.float32)
    hvp_down = jnp.einsum(
        "efr,erd->efd", hidden_dot, cot_rows, preferred_element_type=jnp.float32
    ) + jnp.einsum("efr,erd->efd", hidden, cdot_rows, preferred_element_type=jnp.float32)
    gate_term = (
        (grad_hdot * up_pre + grad_hid * up_dot) * slope + grad_hid * up_pre * curve * gate_dot
    ).astype(jnp.bfloat16)
    up_term = (grad_hdot * active + grad_hid * act_dot).astype(jnp.bfloat16)
    both_terms = jnp.stack([gate_term, up_term], axis=1)
    hvp_gate_up = jnp.einsum("ekfr,erd->ekfd", both_terms, rows, preferred_element_type=jnp.float32)
    return (mixed, hvp_gate_up, hvp_down)


def solution(mesh):
    placed = (
        P(("expert", "dp"), None),
        P(("expert", "dp"), None),
        P(),
        P(("expert", "dp"), None, None),
        P("expert", None, "dp", None),
        P("expert", "dp", None),
        P("expert", None, "dp", None),
        P("expert", "dp", None),
    )
    return jax.shard_map(
        local,
        mesh=mesh,
        in_specs=placed,
        out_specs=(
            P(("expert", "dp"), None),
            P("expert", None, "dp", None),
            P("expert", "dp", None),
        ),
        check_vma=False,
    )
```

```python
import math

import jax
import jax.numpy as jnp
from jax import lax
from jax.sharding import PartitionSpec as P


def regroup(block, lead):
    count, total, width = block.shape
    parted = block.reshape(count, lead, total // lead, width)
    return jnp.swapaxes(parted, 0, 1).reshape(lead, count * total // lead, width)


def _perms(n_dp):
    nx = n_dp // 2
    idx = lambda a, b: 2 * (a % nx) + b
    partner = [(idx(a, b), idx(a, 1 - b)) for a in range(nx) for b in range(2)]
    xplus = [(idx(a, b), idx(a + 1, b)) for a in range(nx) for b in range(2)]
    xminus = [(idx(a, b), idx(a - 1, b)) for a in range(nx) for b in range(2)]
    return partner, xplus, xminus


def tree_gather(block):
    partner, xplus, xminus = _perms(lax.axis_size("dp"))
    send = lambda v, perm: lax.ppermute(v, "dp", perm)
    n = block.shape[0]
    h0, h1 = slice(0, n // 2), slice(n // 2, n)
    q2, q3 = slice(n // 2, 3 * n // 4), slice(3 * n // 4, n)
    Pb = send(block, partner)
    L = send(block, xplus)
    R = send(block, xminus)
    O = jnp.concatenate([send(L[h0], xplus), send(R[h1], xminus)])
    PL = jnp.concatenate([send(Pb[h0], xplus), send(L[h1], partner)])
    PR = jnp.concatenate([send(R[h0], partner), send(Pb[h1], xminus)])
    Q = jnp.concatenate([send(O[h0], partner), send(PR[q2], xminus), send(PL[q3], xplus)])
    return jnp.stack([block, Pb, L, R, O, PL, PR, Q])


def tree_scatter_sum(acc):
    partner, xplus, xminus = _perms(lax.axis_size("dp"))
    send = lambda v, perm: lax.ppermute(v.astype(jnp.bfloat16), "dp", perm).astype(jnp.float32)
    n = acc.shape[1]
    h, q = n // 2, 3 * n // 4
    a7 = acc[7]
    a4 = acc[4] + jnp.concatenate([send(a7[:h], partner), jnp.zeros_like(a7[h:])])
    a5 = acc[5] + jnp.concatenate([jnp.zeros_like(a7[:q]), send(a7[q:], xminus)])
    a6 = acc[6] + jnp.concatenate([jnp.zeros_like(a7[:h]), send(a7[h:q], xplus), jnp.zeros_like(a7[q:])])
    a1 = acc[1] + jnp.concatenate([send(a5[:h], xminus), send(a6[h:], xplus)])
    a2 = acc[2] + jnp.concatenate([send(a4[:h], xminus), send(a5[h:], partner)])
    a3 = acc[3] + jnp.concatenate([send(a6[:h], partner), send(a4[h:], xplus)])
    return acc[0] + send(a1, partner) + send(a2, xminus) + send(a3, xplus)


def gather_dp(block):
    k, e, r, d = block.shape
    got = tree_gather(jnp.moveaxis(block, 2, 0))
    return jnp.moveaxis(got.reshape(-1, k, e, d), 0, 2)


def scatter_sum_dp(part):
    n_dp = lax.axis_size("dp")
    k, e, rows, d = part.shape
    blocks = jnp.transpose(part.astype(jnp.float32).reshape(k, e, n_dp, rows // n_dp, d), (2, 3, 0, 1, 4))
    return jnp.transpose(tree_scatter_sum(blocks), (1, 2, 0, 3))


def local(tokens, targets, router, picks, w_gate_up, w_down, v_gate_up, v_down):
    highest = lax.Precision.HIGHEST
    n_exp = lax.axis_size("expert")
    exp_dev = w_down.shape[0]
    onehot = picks.astype(jnp.bfloat16)
    gates = jax.nn.sigmoid(jnp.dot(tokens, router, preferred_element_type=jnp.float32))
    outgoing = jnp.einsum("tec,td->ecd", onehot, tokens, preferred_element_type=jnp.float32).astype(
        jnp.bfloat16
    )
    arrived = lax.all_to_all(outgoing, "expert", split_axis=0, concat_axis=0, tiled=True)
    rows = gather_dp(regroup(arrived, exp_dev)[None])[0]
    scale = 1.0 / math.sqrt(rows.shape[1])
    primal = jnp.einsum("ekfd,erd->ekfr", w_gate_up, rows, preferred_element_type=jnp.float32)
    tangent = jnp.einsum("ekfd,erd->ekfr", v_gate_up, rows, preferred_element_type=jnp.float32)
    gate_pre, up_pre = (primal[:, 0], primal[:, 1])
    gate_dot, up_dot = (tangent[:, 0], tangent[:, 1])
    sigma = jax.nn.sigmoid(gate_pre)
    active = gate_pre * sigma
    slope = sigma * (1.0 + gate_pre * (1.0 - sigma))
    curve = sigma * (1.0 - sigma) * (2.0 + gate_pre * (1.0 - 2.0 * sigma))
    act_dot = slope * gate_dot
    hidden = (active * up_pre).astype(jnp.bfloat16)
    hidden_dot = (act_dot * up_pre + active * up_dot).astype(jnp.bfloat16)
    part_out = jnp.einsum("efr,efd->erd", hidden, w_down, preferred_element_type=jnp.float32)
    part_dot = jnp.einsum(
        "efr,efd->erd", hidden_dot, w_down, preferred_element_type=jnp.float32
    ) + jnp.einsum("efr,efd->erd", hidden, v_down, preferred_element_type=jnp.float32)
    own_both = scatter_sum_dp(jnp.stack([part_out, part_dot]))
    back_both = jnp.stack(
        [regroup(own_both[0].astype(jnp.bfloat16), n_exp), regroup(own_both[1].astype(jnp.bfloat16), n_exp)],
        axis=1,
    )
    ret_both = lax.all_to_all(back_both, "expert", split_axis=0, concat_axis=0, tiled=True)
    ret_out, ret_dot = (ret_both[:, 0], ret_both[:, 1])
    ret_out = ret_out.astype(jnp.float32)
    ret_dot = ret_dot.astype(jnp.float32)
    weighted = picks.astype(jnp.float32) * gates[:, :, None]
    combined = jnp.einsum("tec,ecd->td", weighted, ret_out, precision=highest)
    combined_dot = jnp.einsum("tec,ecd->td", weighted, ret_dot, precision=highest)
    mixed = combined.astype(jnp.bfloat16)
    resid = scale * (combined - targets.astype(jnp.float32))
    resid_dot = scale * combined_dot
    cot_send = jnp.einsum("tec,td->ecd", weighted, resid, precision=highest).astype(jnp.bfloat16)
    cdot_send = jnp.einsum("tec,td->ecd", weighted, resid_dot, precision=highest).astype(
        jnp.bfloat16
    )
    both_got = lax.all_to_all(
        jnp.stack([cot_send, cdot_send], axis=1), "expert", split_axis=0, concat_axis=0, tiled=True
    )
    own_both = jnp.stack([regroup(both_got[:, 0], exp_dev), regroup(both_got[:, 1], exp_dev)])
    both_rows = gather_dp(own_both)
    cot_rows, cdot_rows = (both_rows[0], both_rows[1])
    grad_hid = jnp.einsum("erd,efd->efr", cot_rows, w_down, preferred_element_type=jnp.float32)
    grad_hdot = jnp.einsum(
        "erd,efd->efr", cdot_rows, w_down, preferred_element_type=jnp.float32
    ) + jnp.einsum("erd,efd->efr", cot_rows, v_down, preferred_element_type=jnp.float32)
    hvp_down = jnp.einsum(
        "efr,erd->efd", hidden_dot, cot_rows, preferred_element_type=jnp.float32
    ) + jnp.einsum("efr,erd->efd", hidden, cdot_rows, preferred_element_type=jnp.float32)
    gate_term = (
        (grad_hdot * up_pre + grad_hid * up_dot) * slope + grad_hid * up_pre * curve * gate_dot
    ).astype(jnp.bfloat16)
    up_term = (grad_hdot * active + grad_hid * act_dot).astype(jnp.bfloat16)
    both_terms = jnp.stack([gate_term, up_term], axis=1)
    hvp_gate_up = jnp.einsum("ekfr,erd->ekfd", both_terms, rows, preferred_element_type=jnp.float32)
    return (mixed, hvp_gate_up, hvp_down)


def solution(mesh):
    placed = (
        P(("expert", "dp"), None),
        P(("expert", "dp"), None),
        P(),
        P(("expert", "dp"), None, None),
        P("expert", None, "dp", None),
        P("expert", "dp", None),
        P("expert", None, "dp", None),
        P("expert", "dp", None),
    )
    return jax.shard_map(
        local,
        mesh=mesh,
        in_specs=placed,
        out_specs=(
            P(("expert", "dp"), None),
            P("expert", None, "dp", None),
            P("expert", "dp", None),
        ),
        check_vma=False,
    )
```

```python
import math

import jax
import jax.numpy as jnp
from jax import lax
from jax.sharding import PartitionSpec as P


def regroup(block, lead):
    count, total, width = block.shape
    parted = block.reshape(count, lead, total // lead, width)
    return jnp.swapaxes(parted, 0, 1).reshape(lead, count * total // lead, width)


def _perms(n_dp):
    nx = n_dp // 2
    idx = lambda a, b: 2 * (a % nx) + b
    partner = [(idx(a, b), idx(a, 1 - b)) for a in range(nx) for b in range(2)]
    xplus = [(idx(a, b), idx(a + 1, b)) for a in range(nx) for b in range(2)]
    xminus = [(idx(a, b), idx(a - 1, b)) for a in range(nx) for b in range(2)]
    return partner, xplus, xminus


def tree_gather(block, axis):
    partner, xplus, xminus = _perms(lax.axis_size("dp"))
    send = lambda v, perm: lax.ppermute(v, "dp", perm)
    half = block.shape[axis] // 2
    first = lambda v: lax.slice_in_dim(v, 0, half, axis=axis)
    second = lambda v: lax.slice_in_dim(v, half, v.shape[axis], axis=axis)
    Pb = send(block, partner)
    L = send(block, xplus)
    R = send(block, xminus)
    O = jnp.concatenate([send(first(L), xplus), send(second(R), xminus)], axis=axis)
    PL = send(Pb, xplus)
    PR = send(Pb, xminus)
    Q = send(O, partner)
    return [block, Pb, L, R, O, PL, PR, Q]


def tree_scatter_sum(acc):
    partner, xplus, xminus = _perms(lax.axis_size("dp"))
    send = lambda v, perm: lax.ppermute(v.astype(jnp.bfloat16), "dp", perm).astype(jnp.float32)
    half = acc[0].shape[0] // 2
    a4 = acc[4] + send(acc[7], partner)
    a2 = acc[2] + jnp.concatenate([send(a4[:half], xminus), jnp.zeros_like(a4[half:])])
    a3 = acc[3] + jnp.concatenate([jnp.zeros_like(a4[:half]), send(a4[half:], xplus)])
    a1 = acc[1] + send(acc[5], xminus) + send(acc[6], xplus)
    return acc[0] + send(a1, partner) + send(a2, xminus) + send(a3, xplus)


def forward_group(rows, w_gate_up, w_down, v_gate_up, v_down):
    primal = jnp.einsum("ekfd,erd->ekfr", w_gate_up, rows, preferred_element_type=jnp.float32)
    tangent = jnp.einsum("ekfd,erd->ekfr", v_gate_up, rows, preferred_element_type=jnp.float32)
    gate_pre, up_pre = (primal[:, 0], primal[:, 1])
    gate_dot, up_dot = (tangent[:, 0], tangent[:, 1])
    sigma = jax.nn.sigmoid(gate_pre)
    active = gate_pre * sigma
    slope = sigma * (1.0 + gate_pre * (1.0 - sigma))
    curve = sigma * (1.0 - sigma) * (2.0 + gate_pre * (1.0 - 2.0 * sigma))
    act_dot = slope * gate_dot
    hidden = (active * up_pre).astype(jnp.bfloat16)
    hidden_dot = (act_dot * up_pre + active * up_dot).astype(jnp.bfloat16)
    part_out = jnp.einsum("efr,efd->erd", hidden, w_down, preferred_element_type=jnp.float32)
    part_dot = jnp.einsum(
        "efr,efd->erd", hidden_dot, w_down, preferred_element_type=jnp.float32
    ) + jnp.einsum("efr,efd->erd", hidden, v_down, preferred_element_type=jnp.float32)
    saved = (rows, up_pre, gate_dot, up_dot, active, slope, curve, act_dot, hidden, hidden_dot)
    return jnp.stack([part_out, part_dot]), saved


def backward_group(cot_blocks, saved, w_down, v_down):
    rows, up_pre, gate_dot, up_dot, active, slope, curve, act_dot, hidden, hidden_dot = saved
    both = jnp.concatenate(cot_blocks, axis=2)
    cot_rows, cdot_rows = (both[0], both[1])
    grad_hid = jnp.einsum("erd,efd->efr", cot_rows, w_down, preferred_element_type=jnp.float32)
    grad_hdot = jnp.einsum(
        "erd,efd->efr", cdot_rows, w_down, preferred_element_type=jnp.float32
    ) + jnp.einsum("erd,efd->efr", cot_rows, v_down, preferred_element_type=jnp.float32)
    hvp_down = jnp.einsum(
        "efr,erd->efd", hidden_dot, cot_rows, preferred_element_type=jnp.float32
    ) + jnp.einsum("efr,erd->efd", hidden, cdot_rows, preferred_element_type=jnp.float32)
    gate_term = (
        (grad_hdot * up_pre + grad_hid * up_dot) * slope + grad_hid * up_pre * curve * gate_dot
    ).astype(jnp.bfloat16)
    up_term = (grad_hdot * active + grad_hid * act_dot).astype(jnp.bfloat16)
    both_terms = jnp.stack([gate_term, up_term], axis=1)
    hvp_gate_up = jnp.einsum("ekfr,erd->ekfd", both_terms, rows, preferred_element_type=jnp.float32)
    return hvp_gate_up, hvp_down


def local(tokens, targets, router, picks, w_gate_up, w_down, v_gate_up, v_down):
    highest = lax.Precision.HIGHEST
    n_exp = lax.axis_size("expert")
    exp_dev = w_down.shape[0]
    onehot = picks.astype(jnp.bfloat16)
    gates = jax.nn.sigmoid(jnp.dot(tokens, router, preferred_element_type=jnp.float32))
    outgoing = jnp.einsum("tec,td->ecd", onehot, tokens, preferred_element_type=jnp.float32).astype(
        jnp.bfloat16
    )
    arrived = lax.all_to_all(outgoing, "expert", split_axis=0, concat_axis=0, tiled=True)
    row_blocks = tree_gather(regroup(arrived, exp_dev), 1)
    block_rows = row_blocks[0].shape[1]
    scale = 1.0 / math.sqrt(block_rows * len(row_blocks))
    groups = (row_blocks[:4], row_blocks[4:])
    parts, saved = [], []
    for blocks in groups:
        part, kept = forward_group(jnp.concatenate(blocks, axis=1), w_gate_up, w_down, v_gate_up, v_down)
        parts += [part[:, :, i * block_rows:(i + 1) * block_rows] for i in range(len(blocks))]
        saved.append(kept)
    own_both = tree_scatter_sum(parts)
    back_both = jnp.stack(
        [regroup(own_both[0].astype(jnp.bfloat16), n_exp), regroup(own_both[1].astype(jnp.bfloat16), n_exp)],
        axis=1,
    )
    ret_both = lax.all_to_all(back_both, "expert", split_axis=0, concat_axis=0, tiled=True)
    ret_out, ret_dot = (ret_both[:, 0], ret_both[:, 1])
    ret_out = ret_out.astype(jnp.float32)
    ret_dot = ret_dot.astype(jnp.float32)
    weighted = picks.astype(jnp.float32) * gates[:, :, None]
    combined = jnp.einsum("tec,ecd->td", weighted, ret_out, precision=highest)
    combined_dot = jnp.einsum("tec,ecd->td", weighted, ret_dot, precision=highest)
    mixed = combined.astype(jnp.bfloat16)
    resid = scale * (combined - targets.astype(jnp.float32))
    resid_dot = scale * combined_dot
    cot_send = jnp.einsum("tec,td->ecd", weighted, resid, precision=highest).astype(jnp.bfloat16)
    cdot_send = jnp.einsum("tec,td->ecd", weighted, resid_dot, precision=highest).astype(
        jnp.bfloat16
    )
    both_got = lax.all_to_all(
        jnp.stack([cot_send, cdot_send], axis=1), "expert", split_axis=0, concat_axis=0, tiled=True
    )
    own_both = jnp.stack([regroup(both_got[:, 0], exp_dev), regroup(both_got[:, 1], exp_dev)])
    cot_blocks = tree_gather(own_both, 0)
    hvp_gate_up, hvp_down = backward_group(cot_blocks[:4], saved[0], w_down, v_down)
    late_gate_up, late_down = backward_group(cot_blocks[4:], saved[1], w_down, v_down)
    return (mixed, hvp_gate_up + late_gate_up, hvp_down + late_down)


def solution(mesh):
    placed = (
        P(("expert", "dp"), None),
        P(("expert", "dp"), None),
        P(),
        P(("expert", "dp"), None, None),
        P("expert", None, "dp", None),
        P("expert", "dp", None),
        P("expert", None, "dp", None),
        P("expert", "dp", None),
    )
    return jax.shard_map(
        local,
        mesh=mesh,
        in_specs=placed,
        out_specs=(
            P(("expert", "dp"), None),
            P("expert", None, "dp", None),
            P("expert", "dp", None),
        ),
        check_vma=False,
    )
```

```python
import math

import jax
import jax.numpy as jnp
from jax import lax
from jax.sharding import PartitionSpec as P


def regroup(block, lead):
    count, total, width = block.shape
    parted = block.reshape(count, lead, total // lead, width)
    return jnp.swapaxes(parted, 0, 1).reshape(lead, count * total // lead, width)


def _perms(n_dp):
    nx = n_dp // 2
    idx = lambda a, b: 2 * (a % nx) + b
    partner = [(idx(a, b), idx(a, 1 - b)) for a in range(nx) for b in range(2)]
    xplus = [(idx(a, b), idx(a + 1, b)) for a in range(nx) for b in range(2)]
    xminus = [(idx(a, b), idx(a - 1, b)) for a in range(nx) for b in range(2)]
    return partner, xplus, xminus


def tree_gather(block, axis):
    partner, xplus, xminus = _perms(lax.axis_size("dp"))
    send = lambda v, perm: lax.ppermute(v, "dp", perm)
    half = block.shape[axis] // 2
    first = lambda v: lax.slice_in_dim(v, 0, half, axis=axis)
    second = lambda v: lax.slice_in_dim(v, half, v.shape[axis], axis=axis)
    Pb = send(block, partner)
    L = send(block, xplus)
    R = send(block, xminus)
    O = jnp.concatenate([send(first(L), xplus), send(second(R), xminus)], axis=axis)
    PL = send(Pb, xplus)
    PR = send(Pb, xminus)
    Q = send(O, partner)
    return [block, Pb, L, R, O, PL, PR, Q]


def tree_scatter_sum(acc, axis):
    partner, xplus, xminus = _perms(lax.axis_size("dp"))
    send = lambda v, perm: lax.ppermute(v.astype(jnp.bfloat16), "dp", perm).astype(jnp.float32)
    half = acc[0].shape[axis] // 2
    first = lambda v: lax.slice_in_dim(v, 0, half, axis=axis)
    second = lambda v: lax.slice_in_dim(v, half, v.shape[axis], axis=axis)
    a4 = acc[4] + send(acc[7], partner)
    a2 = acc[2] + jnp.concatenate([send(first(a4), xminus), jnp.zeros_like(second(a4))], axis=axis)
    a3 = acc[3] + jnp.concatenate([jnp.zeros_like(first(a4)), send(second(a4), xplus)], axis=axis)
    a1 = acc[1] + send(acc[5], xminus) + send(acc[6], xplus)
    return acc[0] + send(a1, partner) + send(a2, xminus) + send(a3, xplus)


def forward_group(rows, w_gate_up, w_down, v_gate_up, v_down):
    primal = jnp.einsum("ekfd,erd->ekfr", w_gate_up, rows, preferred_element_type=jnp.float32)
    tangent = jnp.einsum("ekfd,erd->ekfr", v_gate_up, rows, preferred_element_type=jnp.float32)
    gate_pre, up_pre = (primal[:, 0], primal[:, 1])
    gate_dot, up_dot = (tangent[:, 0], tangent[:, 1])
    sigma = jax.nn.sigmoid(gate_pre)
    active = gate_pre * sigma
    slope = sigma * (1.0 + gate_pre * (1.0 - sigma))
    curve = sigma * (1.0 - sigma) * (2.0 + gate_pre * (1.0 - 2.0 * sigma))
    act_dot = slope * gate_dot
    hidden = (active * up_pre).astype(jnp.bfloat16)
    hidden_dot = (act_dot * up_pre + active * up_dot).astype(jnp.bfloat16)
    part_out = jnp.einsum("efr,efd->erd", hidden, w_down, preferred_element_type=jnp.float32)
    part_dot = jnp.einsum(
        "efr,efd->erd", hidden_dot, w_down, preferred_element_type=jnp.float32
    ) + jnp.einsum("efr,efd->erd", hidden, v_down, preferred_element_type=jnp.float32)
    saved = (rows, up_pre, gate_dot, up_dot, active, slope, curve, act_dot, hidden, hidden_dot)
    return jnp.stack([part_out, part_dot]), saved


def backward_group(cot_blocks, cdot_blocks, saved, w_down, v_down):
    rows, up_pre, gate_dot, up_dot, active, slope, curve, act_dot, hidden, hidden_dot = saved
    cot_rows = jnp.concatenate(cot_blocks, axis=1)
    cdot_rows = jnp.concatenate(cdot_blocks, axis=1)
    grad_hid = jnp.einsum("erd,efd->efr", cot_rows, w_down, preferred_element_type=jnp.float32)
    grad_hdot = jnp.einsum(
        "erd,efd->efr", cdot_rows, w_down, preferred_element_type=jnp.float32
    ) + jnp.einsum("erd,efd->efr", cot_rows, v_down, preferred_element_type=jnp.float32)
    hvp_down = jnp.einsum(
        "efr,erd->efd", hidden_dot, cot_rows, preferred_element_type=jnp.float32
    ) + jnp.einsum("efr,erd->efd", hidden, cdot_rows, preferred_element_type=jnp.float32)
    gate_term = (
        (grad_hdot * up_pre + grad_hid * up_dot) * slope + grad_hid * up_pre * curve * gate_dot
    ).astype(jnp.bfloat16)
    up_term = (grad_hdot * active + grad_hid * act_dot).astype(jnp.bfloat16)
    both_terms = jnp.stack([gate_term, up_term], axis=1)
    hvp_gate_up = jnp.einsum("ekfr,erd->ekfd", both_terms, rows, preferred_element_type=jnp.float32)
    return hvp_gate_up, hvp_down


def local(tokens, targets, router, picks, w_gate_up, w_down, v_gate_up, v_down):
    highest = lax.Precision.HIGHEST
    n_exp = lax.axis_size("expert")
    exp_dev = w_down.shape[0]
    onehot = picks.astype(jnp.bfloat16)
    gates = jax.nn.sigmoid(jnp.dot(tokens, router, preferred_element_type=jnp.float32))
    outgoing = jnp.einsum("tec,td->ecd", onehot, tokens, preferred_element_type=jnp.float32).astype(
        jnp.bfloat16
    )
    arrived = lax.all_to_all(outgoing, "expert", split_axis=0, concat_axis=0, tiled=True)
    row_blocks = tree_gather(regroup(arrived, exp_dev), 1)
    block_rows = row_blocks[0].shape[1]
    scale = 1.0 / math.sqrt(block_rows * len(row_blocks))
    groups = (row_blocks[:4], row_blocks[4:])
    parts, saved = [], []
    for blocks in groups:
        part, kept = forward_group(jnp.concatenate(blocks, axis=1), w_gate_up, w_down, v_gate_up, v_down)
        parts += [part[:, :, i * block_rows:(i + 1) * block_rows] for i in range(len(blocks))]
        saved.append(kept)
    own_out = tree_scatter_sum([part[0] for part in parts], 1)
    own_dot = tree_scatter_sum([part[1] for part in parts], 1)
    weighted = picks.astype(jnp.float32) * gates[:, :, None]
    ret_out = lax.all_to_all(
        regroup(own_out.astype(jnp.bfloat16), n_exp), "expert", split_axis=0, concat_axis=0, tiled=True
    )
    combined = jnp.einsum("tec,ecd->td", weighted, ret_out.astype(jnp.float32), precision=highest)
    mixed = combined.astype(jnp.bfloat16)
    resid = scale * (combined - targets.astype(jnp.float32))
    cot_send = jnp.einsum("tec,td->ecd", weighted, resid, precision=highest).astype(jnp.bfloat16)
    cot_got = lax.all_to_all(cot_send, "expert", split_axis=0, concat_axis=0, tiled=True)
    cot_blocks = tree_gather(regroup(cot_got, exp_dev), 1)
    ret_dot = lax.all_to_all(
        regroup(own_dot.astype(jnp.bfloat16), n_exp), "expert", split_axis=0, concat_axis=0, tiled=True
    )
    combined_dot = jnp.einsum("tec,ecd->td", weighted, ret_dot.astype(jnp.float32), precision=highest)
    resid_dot = scale * combined_dot
    cdot_send = jnp.einsum("tec,td->ecd", weighted, resid_dot, precision=highest).astype(
        jnp.bfloat16
    )
    cdot_got = lax.all_to_all(cdot_send, "expert", split_axis=0, concat_axis=0, tiled=True)
    cdot_blocks = tree_gather(regroup(cdot_got, exp_dev), 1)
    hvp_gate_up, hvp_down = backward_group(cot_blocks[:4], cdot_blocks[:4], saved[0], w_down, v_down)
    late_gate_up, late_down = backward_group(cot_blocks[4:], cdot_blocks[4:], saved[1], w_down, v_down)
    return (mixed, hvp_gate_up + late_gate_up, hvp_down + late_down)


def solution(mesh):
    placed = (
        P(("expert", "dp"), None),
        P(("expert", "dp"), None),
        P(),
        P(("expert", "dp"), None, None),
        P("expert", None, "dp", None),
        P("expert", "dp", None),
        P("expert", None, "dp", None),
        P("expert", "dp", None),
    )
    return jax.shard_map(
        local,
        mesh=mesh,
        in_specs=placed,
        out_specs=(
            P(("expert", "dp"), None),
            P("expert", None, "dp", None),
            P("expert", "dp", None),
        ),
        check_vma=False,
    )
```

```python
import math

import jax
import jax.numpy as jnp
from jax import lax
from jax.sharding import PartitionSpec as P


def regroup(block, lead):
    count, total, width = block.shape
    parted = block.reshape(count, lead, total // lead, width)
    return jnp.swapaxes(parted, 0, 1).reshape(lead, count * total // lead, width)


def _perms(n_dp):
    nx = n_dp // 2
    idx = lambda a, b: 2 * (a % nx) + b
    partner = [(idx(a, b), idx(a, 1 - b)) for a in range(nx) for b in range(2)]
    xplus = [(idx(a, b), idx(a + 1, b)) for a in range(nx) for b in range(2)]
    xminus = [(idx(a, b), idx(a - 1, b)) for a in range(nx) for b in range(2)]
    return partner, xplus, xminus


def tree_gather(block, axis):
    partner, xplus, xminus = _perms(lax.axis_size("dp"))
    send = lambda v, perm: lax.ppermute(v, "dp", perm)
    half = block.shape[axis] // 2
    first = lambda v: lax.slice_in_dim(v, 0, half, axis=axis)
    second = lambda v: lax.slice_in_dim(v, half, v.shape[axis], axis=axis)
    Pb = send(block, partner)
    L = send(block, xplus)
    R = send(block, xminus)
    O = jnp.concatenate([send(first(L), xplus), send(second(R), xminus)], axis=axis)
    PL = send(Pb, xplus)
    PR = send(Pb, xminus)
    Q = send(O, partner)
    return [block, Pb, L, R, O, PL, PR, Q]


def tree_scatter_sum(acc):
    partner, xplus, xminus = _perms(lax.axis_size("dp"))
    send = lambda v, perm: lax.ppermute(v.astype(jnp.bfloat16), "dp", perm).astype(jnp.float32)
    half = acc[0].shape[0] // 2
    a4 = acc[4] + send(acc[7], partner)
    a2 = acc[2] + jnp.concatenate([send(a4[:half], xminus), jnp.zeros_like(a4[half:])])
    a3 = acc[3] + jnp.concatenate([jnp.zeros_like(a4[:half]), send(a4[half:], xplus)])
    a1 = acc[1] + send(acc[5], xminus) + send(acc[6], xplus)
    return acc[0] + send(a1, partner) + send(a2, xminus) + send(a3, xplus)


def forward_group(rows, w_gate_up, w_down, v_gate_up, v_down):
    primal = jnp.einsum("ekfd,erd->ekfr", w_gate_up, rows, preferred_element_type=jnp.float32)
    tangent = jnp.einsum("ekfd,erd->ekfr", v_gate_up, rows, preferred_element_type=jnp.float32)
    gate_pre, up_pre = (primal[:, 0], primal[:, 1])
    gate_dot, up_dot = (tangent[:, 0], tangent[:, 1])
    sigma = jax.nn.sigmoid(gate_pre)
    active = gate_pre * sigma
    slope = sigma * (1.0 + gate_pre * (1.0 - sigma))
    curve = sigma * (1.0 - sigma) * (2.0 + gate_pre * (1.0 - 2.0 * sigma))
    act_dot = slope * gate_dot
    hidden = (active * up_pre).astype(jnp.bfloat16)
    hidden_dot = (act_dot * up_pre + active * up_dot).astype(jnp.bfloat16)
    part_out = jnp.einsum("efr,efd->erd", hidden, w_down, preferred_element_type=jnp.float32)
    part_dot = jnp.einsum(
        "efr,efd->erd", hidden_dot, w_down, preferred_element_type=jnp.float32
    ) + jnp.einsum("efr,efd->erd", hidden, v_down, preferred_element_type=jnp.float32)
    saved = (rows, up_pre, gate_dot, up_dot, active, slope, curve, act_dot, hidden, hidden_dot)
    return jnp.stack([part_out, part_dot]), saved


def backward_group(cot_blocks, saved, w_down, v_down):
    rows, up_pre, gate_dot, up_dot, active, slope, curve, act_dot, hidden, hidden_dot = saved
    both = jnp.concatenate(cot_blocks, axis=2)
    cot_rows, cdot_rows = (both[0], both[1])
    grad_hid = jnp.einsum("erd,efd->efr", cot_rows, w_down, preferred_element_type=jnp.float32)
    grad_hdot = jnp.einsum(
        "erd,efd->efr", cdot_rows, w_down, preferred_element_type=jnp.float32
    ) + jnp.einsum("erd,efd->efr", cot_rows, v_down, preferred_element_type=jnp.float32)
    hvp_down = jnp.einsum(
        "efr,erd->efd", hidden_dot, cot_rows, preferred_element_type=jnp.float32
    ) + jnp.einsum("efr,erd->efd", hidden, cdot_rows, preferred_element_type=jnp.float32)
    gate_term = (
        (grad_hdot * up_pre + grad_hid * up_dot) * slope + grad_hid * up_pre * curve * gate_dot
    ).astype(jnp.bfloat16)
    up_term = (grad_hdot * active + grad_hid * act_dot).astype(jnp.bfloat16)
    both_terms = jnp.stack([gate_term, up_term], axis=1)
    hvp_gate_up = jnp.einsum("ekfr,erd->ekfd", both_terms, rows, preferred_element_type=jnp.float32)
    return hvp_gate_up, hvp_down


def local(tokens, targets, router, picks, w_gate_up, w_down, v_gate_up, v_down):
    highest = lax.Precision.HIGHEST
    n_exp = lax.axis_size("expert")
    exp_dev = w_down.shape[0]
    onehot = picks.astype(jnp.bfloat16)
    gates = jax.nn.sigmoid(jnp.dot(tokens, router, preferred_element_type=jnp.float32))
    outgoing = jnp.einsum("tec,td->ecd", onehot, tokens, preferred_element_type=jnp.float32).astype(
        jnp.bfloat16
    )
    arrived = lax.all_to_all(outgoing, "expert", split_axis=0, concat_axis=0, tiled=True)
    row_blocks = tree_gather(regroup(arrived, exp_dev), 1)
    block_rows = row_blocks[0].shape[1]
    scale = 1.0 / math.sqrt(block_rows * len(row_blocks))
    groups = (row_blocks[:4], row_blocks[4:7], row_blocks[7:])
    parts, saved = [], []
    for blocks in groups:
        part, kept = forward_group(jnp.concatenate(blocks, axis=1), w_gate_up, w_down, v_gate_up, v_down)
        parts += [part[:, :, i * block_rows:(i + 1) * block_rows] for i in range(len(blocks))]
        saved.append(kept)
    own_both = tree_scatter_sum(parts)
    back_both = jnp.stack(
        [regroup(own_both[0].astype(jnp.bfloat16), n_exp), regroup(own_both[1].astype(jnp.bfloat16), n_exp)],
        axis=1,
    )
    ret_both = lax.all_to_all(back_both, "expert", split_axis=0, concat_axis=0, tiled=True)
    ret_out, ret_dot = (ret_both[:, 0], ret_both[:, 1])
    ret_out = ret_out.astype(jnp.float32)
    ret_dot = ret_dot.astype(jnp.float32)
    weighted = picks.astype(jnp.float32) * gates[:, :, None]
    combined = jnp.einsum("tec,ecd->td", weighted, ret_out, precision=highest)
    combined_dot = jnp.einsum("tec,ecd->td", weighted, ret_dot, precision=highest)
    mixed = combined.astype(jnp.bfloat16)
    resid = scale * (combined - targets.astype(jnp.float32))
    resid_dot = scale * combined_dot
    cot_send = jnp.einsum("tec,td->ecd", weighted, resid, precision=highest).astype(jnp.bfloat16)
    cdot_send = jnp.einsum("tec,td->ecd", weighted, resid_dot, precision=highest).astype(
        jnp.bfloat16
    )
    both_got = lax.all_to_all(
        jnp.stack([cot_send, cdot_send], axis=1), "expert", split_axis=0, concat_axis=0, tiled=True
    )
    own_both = jnp.stack([regroup(both_got[:, 0], exp_dev), regroup(both_got[:, 1], exp_dev)])
    cot_blocks = tree_gather(own_both, 0)
    hvp_gate_up, hvp_down = backward_group(cot_blocks[:4], saved[0], w_down, v_down)
    for blocks, kept in ((cot_blocks[4:7], saved[1]), (cot_blocks[7:], saved[2])):
        more_gate_up, more_down = backward_group(blocks, kept, w_down, v_down)
        hvp_gate_up, hvp_down = (hvp_gate_up + more_gate_up, hvp_down + more_down)
    return (mixed, hvp_gate_up, hvp_down)


def solution(mesh):
    placed = (
        P(("expert", "dp"), None),
        P(("expert", "dp"), None),
        P(),
        P(("expert", "dp"), None, None),
        P("expert", None, "dp", None),
        P("expert", "dp", None),
        P("expert", None, "dp", None),
        P("expert", "dp", None),
    )
    return jax.shard_map(
        local,
        mesh=mesh,
        in_specs=placed,
        out_specs=(
            P(("expert", "dp"), None),
            P("expert", None, "dp", None),
            P("expert", "dp", None),
        ),
        check_vma=False,
    )
```

```python
import math

import jax
import jax.numpy as jnp
from jax import lax
from jax.sharding import PartitionSpec as P


def regroup(block, lead):
    count, total, width = block.shape
    parted = block.reshape(count, lead, total // lead, width)
    return jnp.swapaxes(parted, 0, 1).reshape(lead, count * total // lead, width)


def _perms(n_dp):
    nx = n_dp // 2
    idx = lambda a, b: 2 * (a % nx) + b
    partner = [(idx(a, b), idx(a, 1 - b)) for a in range(nx) for b in range(2)]
    xplus = [(idx(a, b), idx(a + 1, b)) for a in range(nx) for b in range(2)]
    xminus = [(idx(a, b), idx(a - 1, b)) for a in range(nx) for b in range(2)]
    return partner, xplus, xminus


def tree_gather(block, axis):
    partner, xplus, xminus = _perms(lax.axis_size("dp"))
    send = lambda v, perm: lax.ppermute(v, "dp", perm)
    half = block.shape[axis] // 2
    first = lambda v: lax.slice_in_dim(v, 0, half, axis=axis)
    second = lambda v: lax.slice_in_dim(v, half, v.shape[axis], axis=axis)
    Pb = send(block, partner)
    L = send(block, xplus)
    R = send(block, xminus)
    O = jnp.concatenate([send(first(L), xplus), send(second(R), xminus)], axis=axis)
    PL = send(Pb, xplus)
    PR = send(Pb, xminus)
    Q = send(O, partner)
    return [block, Pb, L, R, O, PL, PR, Q]


def tree_scatter_sum(acc, axis):
    partner, xplus, xminus = _perms(lax.axis_size("dp"))
    send = lambda v, perm: lax.ppermute(v.astype(jnp.bfloat16), "dp", perm).astype(jnp.float32)
    half = acc[0].shape[axis] // 2
    first = lambda v: lax.slice_in_dim(v, 0, half, axis=axis)
    second = lambda v: lax.slice_in_dim(v, half, v.shape[axis], axis=axis)
    a4 = acc[4] + send(acc[7], partner)
    a2 = acc[2] + jnp.concatenate([send(first(a4), xminus), jnp.zeros_like(second(a4))], axis=axis)
    a3 = acc[3] + jnp.concatenate([jnp.zeros_like(first(a4)), send(second(a4), xplus)], axis=axis)
    a1 = acc[1] + send(acc[5], xminus) + send(acc[6], xplus)
    return acc[0] + send(a1, partner) + send(a2, xminus) + send(a3, xplus)


def forward_group(rows, w_gate_up, w_down, v_gate_up, v_down):
    primal = jnp.einsum("ekfd,erd->ekfr", w_gate_up, rows, preferred_element_type=jnp.float32)
    tangent = jnp.einsum("ekfd,erd->ekfr", v_gate_up, rows, preferred_element_type=jnp.float32)
    gate_pre, up_pre = (primal[:, 0], primal[:, 1])
    gate_dot, up_dot = (tangent[:, 0], tangent[:, 1])
    sigma = jax.nn.sigmoid(gate_pre)
    active = gate_pre * sigma
    slope = sigma * (1.0 + gate_pre * (1.0 - sigma))
    curve = sigma * (1.0 - sigma) * (2.0 + gate_pre * (1.0 - 2.0 * sigma))
    act_dot = slope * gate_dot
    hidden = (active * up_pre).astype(jnp.bfloat16)
    hidden_dot = (act_dot * up_pre + active * up_dot).astype(jnp.bfloat16)
    part_out = jnp.einsum("efr,efd->erd", hidden, w_down, preferred_element_type=jnp.float32)
    part_dot = jnp.einsum(
        "efr,efd->erd", hidden_dot, w_down, preferred_element_type=jnp.float32
    ) + jnp.einsum("efr,efd->erd", hidden, v_down, preferred_element_type=jnp.float32)
    saved = (rows, up_pre, gate_dot, up_dot, active, slope, curve, act_dot, hidden, hidden_dot)
    return jnp.stack([part_out, part_dot]), saved


def backward_group(cot_blocks, cdot_blocks, saved, w_down, v_down):
    rows, up_pre, gate_dot, up_dot, active, slope, curve, act_dot, hidden, hidden_dot = saved
    cot_rows = jnp.concatenate(cot_blocks, axis=1)
    cdot_rows = jnp.concatenate(cdot_blocks, axis=1)
    grad_hid = jnp.einsum("erd,efd->efr", cot_rows, w_down, preferred_element_type=jnp.float32)
    grad_hdot = jnp.einsum(
        "erd,efd->efr", cdot_rows, w_down, preferred_element_type=jnp.float32
    ) + jnp.einsum("erd,efd->efr", cot_rows, v_down, preferred_element_type=jnp.float32)
    hvp_down = jnp.einsum(
        "efr,erd->efd", hidden_dot, cot_rows, preferred_element_type=jnp.float32
    ) + jnp.einsum("efr,erd->efd", hidden, cdot_rows, preferred_element_type=jnp.float32)
    gate_term = (
        (grad_hdot * up_pre + grad_hid * up_dot) * slope + grad_hid * up_pre * curve * gate_dot
    ).astype(jnp.bfloat16)
    up_term = (grad_hdot * active + grad_hid * act_dot).astype(jnp.bfloat16)
    both_terms = jnp.stack([gate_term, up_term], axis=1)
    hvp_gate_up = jnp.einsum("ekfr,erd->ekfd", both_terms, rows, preferred_element_type=jnp.float32)
    return hvp_gate_up, hvp_down


def local(tokens, targets, router, picks, w_gate_up, w_down, v_gate_up, v_down):
    highest = lax.Precision.HIGHEST
    n_exp = lax.axis_size("expert")
    exp_dev = w_down.shape[0]
    onehot = picks.astype(jnp.bfloat16)
    gates = jax.nn.sigmoid(jnp.dot(tokens, router, preferred_element_type=jnp.float32))
    outgoing = jnp.einsum("tec,td->ecd", onehot, tokens, preferred_element_type=jnp.float32).astype(
        jnp.bfloat16
    )
    arrived = lax.all_to_all(outgoing, "expert", split_axis=0, concat_axis=0, tiled=True)
    row_blocks = tree_gather(regroup(arrived, exp_dev), 1)
    block_rows = row_blocks[0].shape[1]
    scale = 1.0 / math.sqrt(block_rows * len(row_blocks))
    groups = (row_blocks[:4], row_blocks[4:])
    parts, saved = [], []
    for blocks in groups:
        part, kept = forward_group(jnp.concatenate(blocks, axis=1), w_gate_up, w_down, v_gate_up, v_down)
        parts += [part[:, :, i * block_rows:(i + 1) * block_rows] for i in range(len(blocks))]
        saved.append(kept)
    own_out = tree_scatter_sum([part[0] for part in parts], 1)
    dot_parts, own_out = lax.optimization_barrier(([part[1] for part in parts], own_out))
    own_dot = tree_scatter_sum(dot_parts, 1)
    weighted = picks.astype(jnp.float32) * gates[:, :, None]
    ret_out = lax.all_to_all(
        regroup(own_out.astype(jnp.bfloat16), n_exp), "expert", split_axis=0, concat_axis=0, tiled=True
    )
    combined = jnp.einsum("tec,ecd->td", weighted, ret_out.astype(jnp.float32), precision=highest)
    mixed = combined.astype(jnp.bfloat16)
    resid = scale * (combined - targets.astype(jnp.float32))
    cot_send = jnp.einsum("tec,td->ecd", weighted, resid, precision=highest).astype(jnp.bfloat16)
    cot_got = lax.all_to_all(cot_send, "expert", split_axis=0, concat_axis=0, tiled=True)
    cot_blocks = tree_gather(regroup(cot_got, exp_dev), 1)
    dot_back, cot_got = lax.optimization_barrier((regroup(own_dot.astype(jnp.bfloat16), n_exp), cot_got))
    ret_dot = lax.all_to_all(dot_back, "expert", split_axis=0, concat_axis=0, tiled=True)
    combined_dot = jnp.einsum("tec,ecd->td", weighted, ret_dot.astype(jnp.float32), precision=highest)
    resid_dot = scale * combined_dot
    cdot_send = jnp.einsum("tec,td->ecd", weighted, resid_dot, precision=highest).astype(
        jnp.bfloat16
    )
    cdot_got = lax.all_to_all(cdot_send, "expert", split_axis=0, concat_axis=0, tiled=True)
    cdot_blocks = tree_gather(regroup(cdot_got, exp_dev), 1)
    hvp_gate_up, hvp_down = backward_group(cot_blocks[:4], cdot_blocks[:4], saved[0], w_down, v_down)
    late_gate_up, late_down = backward_group(cot_blocks[4:], cdot_blocks[4:], saved[1], w_down, v_down)
    return (mixed, hvp_gate_up + late_gate_up, hvp_down + late_down)


def solution(mesh):
    placed = (
        P(("expert", "dp"), None),
        P(("expert", "dp"), None),
        P(),
        P(("expert", "dp"), None, None),
        P("expert", None, "dp", None),
        P("expert", "dp", None),
        P("expert", None, "dp", None),
        P("expert", "dp", None),
    )
    return jax.shard_map(
        local,
        mesh=mesh,
        in_specs=placed,
        out_specs=(
            P(("expert", "dp"), None),
            P("expert", None, "dp", None),
            P("expert", "dp", None),
        ),
        check_vma=False,
    )
```

```python
import math

import jax
import jax.numpy as jnp
from jax import lax
from jax.sharding import PartitionSpec as P


def regroup(block, lead):
    count, total, width = block.shape
    parted = block.reshape(count, lead, total // lead, width)
    return jnp.swapaxes(parted, 0, 1).reshape(lead, count * total // lead, width)


def _perms(n_dp):
    nx = n_dp // 2
    idx = lambda a, b: 2 * (a % nx) + b
    partner = [(idx(a, b), idx(a, 1 - b)) for a in range(nx) for b in range(2)]
    xplus = [(idx(a, b), idx(a + 1, b)) for a in range(nx) for b in range(2)]
    xminus = [(idx(a, b), idx(a - 1, b)) for a in range(nx) for b in range(2)]
    return partner, xplus, xminus


def tree_gather(block, axis):
    partner, xplus, xminus = _perms(lax.axis_size("dp"))
    send = lambda v, perm: lax.ppermute(v, "dp", perm)
    half = block.shape[axis] // 2
    first = lambda v: lax.slice_in_dim(v, 0, half, axis=axis)
    second = lambda v: lax.slice_in_dim(v, half, v.shape[axis], axis=axis)
    Pb = send(block, partner)
    L = send(block, xplus)
    R = send(block, xminus)
    O = jnp.concatenate([send(first(L), xplus), send(second(R), xminus)], axis=axis)
    PL = send(Pb, xplus)
    PR = send(Pb, xminus)
    Q = send(O, partner)
    return [block, Pb, L, R, O, PL, PR, Q]


def tree_scatter_sum(acc, axis):
    partner, xplus, xminus = _perms(lax.axis_size("dp"))
    send = lambda v, perm: lax.ppermute(v.astype(jnp.bfloat16), "dp", perm).astype(jnp.float32)
    half = acc[0].shape[axis] // 2
    first = lambda v: lax.slice_in_dim(v, 0, half, axis=axis)
    second = lambda v: lax.slice_in_dim(v, half, v.shape[axis], axis=axis)
    a4 = acc[4] + send(acc[7], partner)
    a2 = acc[2] + jnp.concatenate([send(first(a4), xminus), jnp.zeros_like(second(a4))], axis=axis)
    a3 = acc[3] + jnp.concatenate([jnp.zeros_like(first(a4)), send(second(a4), xplus)], axis=axis)
    a1 = acc[1] + send(acc[5], xminus) + send(acc[6], xplus)
    return acc[0] + send(a1, partner) + send(a2, xminus) + send(a3, xplus)


def forward_group(rows, w_gate_up, w_down, v_gate_up, v_down):
    primal = jnp.einsum("ekfd,erd->ekfr", w_gate_up, rows, preferred_element_type=jnp.float32)
    tangent = jnp.einsum("ekfd,erd->ekfr", v_gate_up, rows, preferred_element_type=jnp.float32)
    gate_pre, up_pre = (primal[:, 0], primal[:, 1])
    gate_dot, up_dot = (tangent[:, 0], tangent[:, 1])
    sigma = jax.nn.sigmoid(gate_pre)
    active = gate_pre * sigma
    slope = sigma * (1.0 + gate_pre * (1.0 - sigma))
    curve = sigma * (1.0 - sigma) * (2.0 + gate_pre * (1.0 - 2.0 * sigma))
    act_dot = slope * gate_dot
    hidden = (active * up_pre).astype(jnp.bfloat16)
    hidden_dot = (act_dot * up_pre + active * up_dot).astype(jnp.bfloat16)
    part_out = jnp.einsum("efr,efd->erd", hidden, w_down, preferred_element_type=jnp.float32)
    part_dot = jnp.einsum(
        "efr,efd->erd", hidden_dot, w_down, preferred_element_type=jnp.float32
    ) + jnp.einsum("efr,efd->erd", hidden, v_down, preferred_element_type=jnp.float32)
    saved = (rows, up_pre, gate_dot, up_dot, active, slope, curve, act_dot, hidden, hidden_dot)
    return jnp.stack([part_out, part_dot]), saved


def backward_group(cot_blocks, cdot_blocks, saved, w_down, v_down):
    rows, up_pre, gate_dot, up_dot, active, slope, curve, act_dot, hidden, hidden_dot = saved
    cot_rows = jnp.concatenate(cot_blocks, axis=1)
    grad_hid = jnp.einsum("erd,efd->efr", cot_rows, w_down, preferred_element_type=jnp.float32)
    hdot_early = jnp.einsum("erd,efd->efr", cot_rows, v_down, preferred_element_type=jnp.float32)
    down_early = jnp.einsum("efr,erd->efd", hidden_dot, cot_rows, preferred_element_type=jnp.float32)
    cdot_rows = jnp.concatenate(cdot_blocks, axis=1)
    grad_hdot = jnp.einsum("erd,efd->efr", cdot_rows, w_down, preferred_element_type=jnp.float32) + hdot_early
    hvp_down = down_early + jnp.einsum("efr,erd->efd", hidden, cdot_rows, preferred_element_type=jnp.float32)
    gate_term = (
        (grad_hdot * up_pre + grad_hid * up_dot) * slope + grad_hid * up_pre * curve * gate_dot
    ).astype(jnp.bfloat16)
    up_term = (grad_hdot * active + grad_hid * act_dot).astype(jnp.bfloat16)
    both_terms = jnp.stack([gate_term, up_term], axis=1)
    hvp_gate_up = jnp.einsum("ekfr,erd->ekfd", both_terms, rows, preferred_element_type=jnp.float32)
    return hvp_gate_up, hvp_down


def local(tokens, targets, router, picks, w_gate_up, w_down, v_gate_up, v_down):
    highest = lax.Precision.HIGHEST
    n_exp = lax.axis_size("expert")
    exp_dev = w_down.shape[0]
    onehot = picks.astype(jnp.bfloat16)
    gates = jax.nn.sigmoid(jnp.dot(tokens, router, preferred_element_type=jnp.float32))
    outgoing = jnp.einsum("tec,td->ecd", onehot, tokens, preferred_element_type=jnp.float32).astype(
        jnp.bfloat16
    )
    arrived = lax.all_to_all(outgoing, "expert", split_axis=0, concat_axis=0, tiled=True)
    row_blocks = tree_gather(regroup(arrived, exp_dev), 1)
    block_rows = row_blocks[0].shape[1]
    scale = 1.0 / math.sqrt(block_rows * len(row_blocks))
    groups = (row_blocks[:4], row_blocks[4:])
    parts, saved = [], []
    for blocks in groups:
        part, kept = forward_group(jnp.concatenate(blocks, axis=1), w_gate_up, w_down, v_gate_up, v_down)
        parts += [part[:, :, i * block_rows:(i + 1) * block_rows] for i in range(len(blocks))]
        saved.append(kept)
    own_out = tree_scatter_sum([part[0] for part in parts], 1)
    dot_parts, own_out = lax.optimization_barrier(([part[1] for part in parts], own_out))
    own_dot = tree_scatter_sum(dot_parts, 1)
    weighted = picks.astype(jnp.float32) * gates[:, :, None]
    ret_out = lax.all_to_all(
        regroup(own_out.astype(jnp.bfloat16), n_exp), "expert", split_axis=0, concat_axis=0, tiled=True
    )
    combined = jnp.einsum("tec,ecd->td", weighted, ret_out.astype(jnp.float32), precision=highest)
    mixed = combined.astype(jnp.bfloat16)
    resid = scale * (combined - targets.astype(jnp.float32))
    cot_send = jnp.einsum("tec,td->ecd", weighted, resid, precision=highest).astype(jnp.bfloat16)
    cot_got = lax.all_to_all(cot_send, "expert", split_axis=0, concat_axis=0, tiled=True)
    cot_blocks = tree_gather(regroup(cot_got, exp_dev), 1)
    dot_back, cot_got = lax.optimization_barrier((regroup(own_dot.astype(jnp.bfloat16), n_exp), cot_got))
    ret_dot = lax.all_to_all(dot_back, "expert", split_axis=0, concat_axis=0, tiled=True)
    combined_dot = jnp.einsum("tec,ecd->td", weighted, ret_dot.astype(jnp.float32), precision=highest)
    resid_dot = scale * combined_dot
    cdot_send = jnp.einsum("tec,td->ecd", weighted, resid_dot, precision=highest).astype(
        jnp.bfloat16
    )
    cdot_got = lax.all_to_all(cdot_send, "expert", split_axis=0, concat_axis=0, tiled=True)
    cdot_blocks = tree_gather(regroup(cdot_got, exp_dev), 1)
    hvp_gate_up, hvp_down = backward_group(cot_blocks[:4], cdot_blocks[:4], saved[0], w_down, v_down)
    late_gate_up, late_down = backward_group(cot_blocks[4:], cdot_blocks[4:], saved[1], w_down, v_down)
    return (mixed, hvp_gate_up + late_gate_up, hvp_down + late_down)


def solution(mesh):
    placed = (
        P(("expert", "dp"), None),
        P(("expert", "dp"), None),
        P(),
        P(("expert", "dp"), None, None),
        P("expert", None, "dp", None),
        P("expert", "dp", None),
        P("expert", None, "dp", None),
        P("expert", "dp", None),
    )
    return jax.shard_map(
        local,
        mesh=mesh,
        in_specs=placed,
        out_specs=(
            P(("expert", "dp"), None),
            P("expert", None, "dp", None),
            P("expert", "dp", None),
        ),
        check_vma=False,
    )
```

```python
import math

import jax
import jax.numpy as jnp
from jax import lax
from jax.sharding import PartitionSpec as P


def regroup(block, lead):
    count, total, width = block.shape
    parted = block.reshape(count, lead, total // lead, width)
    return jnp.swapaxes(parted, 0, 1).reshape(lead, count * total // lead, width)


def _perms(n_dp):
    nx = n_dp // 2
    idx = lambda a, b: 2 * (a % nx) + b
    partner = [(idx(a, b), idx(a, 1 - b)) for a in range(nx) for b in range(2)]
    xplus = [(idx(a, b), idx(a + 1, b)) for a in range(nx) for b in range(2)]
    xminus = [(idx(a, b), idx(a - 1, b)) for a in range(nx) for b in range(2)]
    return partner, xplus, xminus


def tree_gather(block, axis):
    partner, xplus, xminus = _perms(lax.axis_size("dp"))
    send = lambda v, perm: lax.ppermute(v, "dp", perm)
    half = block.shape[axis] // 2
    first = lambda v: lax.slice_in_dim(v, 0, half, axis=axis)
    second = lambda v: lax.slice_in_dim(v, half, v.shape[axis], axis=axis)
    Pb = send(block, partner)
    L = send(block, xplus)
    R = send(block, xminus)
    O = jnp.concatenate([send(first(L), xplus), send(second(R), xminus)], axis=axis)
    PL = send(Pb, xplus)
    PR = send(Pb, xminus)
    Q = send(O, partner)
    return [block, Pb, L, R, O, PL, PR, Q]


def tree_scatter_sum(acc, axis):
    partner, xplus, xminus = _perms(lax.axis_size("dp"))
    send = lambda v, perm: lax.ppermute(v.astype(jnp.bfloat16), "dp", perm).astype(jnp.float32)
    half = acc[0].shape[axis] // 2
    first = lambda v: lax.slice_in_dim(v, 0, half, axis=axis)
    second = lambda v: lax.slice_in_dim(v, half, v.shape[axis], axis=axis)
    a4 = acc[4] + send(acc[7], partner)
    a2 = acc[2] + jnp.concatenate([send(first(a4), xminus), jnp.zeros_like(second(a4))], axis=axis)
    a3 = acc[3] + jnp.concatenate([jnp.zeros_like(first(a4)), send(second(a4), xplus)], axis=axis)
    a1 = acc[1] + send(acc[5], xminus) + send(acc[6], xplus)
    return acc[0] + send(a1, partner) + send(a2, xminus) + send(a3, xplus)


def forward_group(rows, w_gate_up, w_down, v_gate_up, v_down):
    primal = jnp.einsum("ekfd,erd->ekfr", w_gate_up, rows, preferred_element_type=jnp.float32)
    tangent = jnp.einsum("ekfd,erd->ekfr", v_gate_up, rows, preferred_element_type=jnp.float32)
    gate_pre, up_pre = (primal[:, 0], primal[:, 1])
    gate_dot, up_dot = (tangent[:, 0], tangent[:, 1])
    sigma = jax.nn.sigmoid(gate_pre)
    active = gate_pre * sigma
    slope = sigma * (1.0 + gate_pre * (1.0 - sigma))
    curve = sigma * (1.0 - sigma) * (2.0 + gate_pre * (1.0 - 2.0 * sigma))
    act_dot = slope * gate_dot
    hidden = (active * up_pre).astype(jnp.bfloat16)
    hidden_dot = (act_dot * up_pre + active * up_dot).astype(jnp.bfloat16)
    part_out = jnp.einsum("efr,efd->erd", hidden, w_down, preferred_element_type=jnp.float32)
    part_dot = jnp.einsum(
        "efr,efd->erd", hidden_dot, w_down, preferred_element_type=jnp.float32
    ) + jnp.einsum("efr,efd->erd", hidden, v_down, preferred_element_type=jnp.float32)
    saved = (rows, up_pre, gate_dot, up_dot, active, slope, curve, act_dot, hidden, hidden_dot)
    return jnp.stack([part_out, part_dot]), saved


def backward_group(cot_blocks, cdot_blocks, saved, w_down, v_down):
    rows, up_pre, gate_dot, up_dot, active, slope, curve, act_dot, hidden, hidden_dot = saved
    cot_rows = jnp.concatenate(cot_blocks, axis=1)
    grad_hid = jnp.einsum("erd,efd->efr", cot_rows, w_down, preferred_element_type=jnp.float32)
    hdot_early = jnp.einsum("erd,efd->efr", cot_rows, v_down, preferred_element_type=jnp.float32)
    down_early = jnp.einsum("efr,erd->efd", hidden_dot, cot_rows, preferred_element_type=jnp.float32)
    cdot_rows = jnp.concatenate(cdot_blocks, axis=1)
    grad_hdot = jnp.einsum("erd,efd->efr", cdot_rows, w_down, preferred_element_type=jnp.float32) + hdot_early
    hvp_down = down_early + jnp.einsum("efr,erd->efd", hidden, cdot_rows, preferred_element_type=jnp.float32)
    gate_term = (
        (grad_hdot * up_pre + grad_hid * up_dot) * slope + grad_hid * up_pre * curve * gate_dot
    ).astype(jnp.bfloat16)
    up_term = (grad_hdot * active + grad_hid * act_dot).astype(jnp.bfloat16)
    both_terms = jnp.stack([gate_term, up_term], axis=1)
    hvp_gate_up = jnp.einsum("ekfr,erd->ekfd", both_terms, rows, preferred_element_type=jnp.float32)
    return hvp_gate_up, hvp_down


def local(tokens, targets, router, picks, w_gate_up, w_down, v_gate_up, v_down):
    highest = lax.Precision.HIGHEST
    n_exp = lax.axis_size("expert")
    exp_dev = w_down.shape[0]
    onehot = picks.astype(jnp.bfloat16)
    gates = jax.nn.sigmoid(jnp.dot(tokens, router, preferred_element_type=jnp.float32))
    outgoing = jnp.einsum("tec,td->ecd", onehot, tokens, preferred_element_type=jnp.float32).astype(
        jnp.bfloat16
    )
    arrived = lax.all_to_all(outgoing, "expert", split_axis=0, concat_axis=0, tiled=True)
    row_blocks = tree_gather(regroup(arrived, exp_dev), 1)
    block_rows = row_blocks[0].shape[1]
    scale = 1.0 / math.sqrt(block_rows * len(row_blocks))
    groups = (row_blocks[:4], row_blocks[4:7], row_blocks[7:])
    parts, saved = [], []
    for blocks in groups:
        part, kept = forward_group(jnp.concatenate(blocks, axis=1), w_gate_up, w_down, v_gate_up, v_down)
        parts += [part[:, :, i * block_rows:(i + 1) * block_rows] for i in range(len(blocks))]
        saved.append(kept)
    own_out = tree_scatter_sum([part[0] for part in parts], 1)
    dot_parts, own_out = lax.optimization_barrier(([part[1] for part in parts], own_out))
    own_dot = tree_scatter_sum(dot_parts, 1)
    weighted = picks.astype(jnp.float32) * gates[:, :, None]
    ret_out = lax.all_to_all(
        regroup(own_out.astype(jnp.bfloat16), n_exp), "expert", split_axis=0, concat_axis=0, tiled=True
    )
    combined = jnp.einsum("tec,ecd->td", weighted, ret_out.astype(jnp.float32), precision=highest)
    mixed = combined.astype(jnp.bfloat16)
    resid = scale * (combined - targets.astype(jnp.float32))
    cot_send = jnp.einsum("tec,td->ecd", weighted, resid, precision=highest).astype(jnp.bfloat16)
    cot_got = lax.all_to_all(cot_send, "expert", split_axis=0, concat_axis=0, tiled=True)
    cot_blocks = tree_gather(regroup(cot_got, exp_dev), 1)
    dot_back, cot_got = lax.optimization_barrier((regroup(own_dot.astype(jnp.bfloat16), n_exp), cot_got))
    ret_dot = lax.all_to_all(dot_back, "expert", split_axis=0, concat_axis=0, tiled=True)
    combined_dot = jnp.einsum("tec,ecd->td", weighted, ret_dot.astype(jnp.float32), precision=highest)
    resid_dot = scale * combined_dot
    cdot_send = jnp.einsum("tec,td->ecd", weighted, resid_dot, precision=highest).astype(
        jnp.bfloat16
    )
    cdot_got = lax.all_to_all(cdot_send, "expert", split_axis=0, concat_axis=0, tiled=True)
    cdot_blocks = tree_gather(regroup(cdot_got, exp_dev), 1)
    hvp_gate_up, hvp_down = backward_group(cot_blocks[:4], cdot_blocks[:4], saved[0], w_down, v_down)
    for part, kept in zip((slice(4, 7), slice(7, 8)), saved[1:]):
        more_gate_up, more_down = backward_group(cot_blocks[part], cdot_blocks[part], kept, w_down, v_down)
        hvp_gate_up, hvp_down = (hvp_gate_up + more_gate_up, hvp_down + more_down)
    return (mixed, hvp_gate_up, hvp_down)


def solution(mesh):
    placed = (
        P(("expert", "dp"), None),
        P(("expert", "dp"), None),
        P(),
        P(("expert", "dp"), None, None),
        P("expert", None, "dp", None),
        P("expert", "dp", None),
        P("expert", None, "dp", None),
        P("expert", "dp", None),
    )
    return jax.shard_map(
        local,
        mesh=mesh,
        in_specs=placed,
        out_specs=(
            P(("expert", "dp"), None),
            P("expert", None, "dp", None),
            P("expert", "dp", None),
        ),
        check_vma=False,
    )
```

```python
import math

import jax
import jax.numpy as jnp
from jax import lax
from jax.sharding import PartitionSpec as P


def regroup(block, lead):
    count, total, width = block.shape
    parted = block.reshape(count, lead, total // lead, width)
    return jnp.swapaxes(parted, 0, 1).reshape(lead, count * total // lead, width)


def _perms(n_dp):
    nx = n_dp // 2
    idx = lambda a, b: 2 * (a % nx) + b
    partner = [(idx(a, b), idx(a, 1 - b)) for a in range(nx) for b in range(2)]
    xplus = [(idx(a, b), idx(a + 1, b)) for a in range(nx) for b in range(2)]
    xminus = [(idx(a, b), idx(a - 1, b)) for a in range(nx) for b in range(2)]
    return partner, xplus, xminus


def tree_gather(block, axis):
    partner, xplus, xminus = _perms(lax.axis_size("dp"))
    send = lambda v, perm: lax.ppermute(v, "dp", perm)
    half = block.shape[axis] // 2
    first = lambda v: lax.slice_in_dim(v, 0, half, axis=axis)
    second = lambda v: lax.slice_in_dim(v, half, v.shape[axis], axis=axis)
    Pb = send(block, partner)
    L = send(block, xplus)
    R = send(block, xminus)
    O = jnp.concatenate([send(first(L), xplus), send(second(R), xminus)], axis=axis)
    PL = send(Pb, xplus)
    PR = send(Pb, xminus)
    Q = send(O, partner)
    return [block, Pb, L, R, O, PL, PR, Q]


def tree_scatter_sum(acc, axis):
    partner, xplus, xminus = _perms(lax.axis_size("dp"))
    send = lambda v, perm: lax.ppermute(v.astype(jnp.bfloat16), "dp", perm).astype(jnp.float32)
    half = acc[0].shape[axis] // 2
    first = lambda v: lax.slice_in_dim(v, 0, half, axis=axis)
    second = lambda v: lax.slice_in_dim(v, half, v.shape[axis], axis=axis)
    a4 = acc[4] + send(acc[7], partner)
    a2 = acc[2] + jnp.concatenate([send(first(a4), xminus), jnp.zeros_like(second(a4))], axis=axis)
    a3 = acc[3] + jnp.concatenate([jnp.zeros_like(first(a4)), send(second(a4), xplus)], axis=axis)
    a1 = acc[1] + send(acc[5], xminus) + send(acc[6], xplus)
    return acc[0] + send(a1, partner) + send(a2, xminus) + send(a3, xplus)


def forward_group(rows, w_gate_up, w_down, v_gate_up, v_down):
    primal = jnp.einsum("ekfd,erd->ekfr", w_gate_up, rows, preferred_element_type=jnp.float32)
    tangent = jnp.einsum("ekfd,erd->ekfr", v_gate_up, rows, preferred_element_type=jnp.float32)
    gate_pre, up_pre = (primal[:, 0], primal[:, 1])
    gate_dot, up_dot = (tangent[:, 0], tangent[:, 1])
    sigma = jax.nn.sigmoid(gate_pre)
    active = gate_pre * sigma
    slope = sigma * (1.0 + gate_pre * (1.0 - sigma))
    curve = sigma * (1.0 - sigma) * (2.0 + gate_pre * (1.0 - 2.0 * sigma))
    act_dot = slope * gate_dot
    hidden = (active * up_pre).astype(jnp.bfloat16)
    hidden_dot = (act_dot * up_pre + active * up_dot).astype(jnp.bfloat16)
    part_out = jnp.einsum("efr,efd->erd", hidden, w_down, preferred_element_type=jnp.float32)
    part_dot = jnp.einsum(
        "efr,efd->erd", hidden_dot, w_down, preferred_element_type=jnp.float32
    ) + jnp.einsum("efr,efd->erd", hidden, v_down, preferred_element_type=jnp.float32)
    saved = (rows, up_pre, gate_dot, up_dot, active, slope, curve, act_dot, hidden, hidden_dot)
    return jnp.stack([part_out, part_dot]), saved


def backward_group(cot_blocks, cdot_blocks, saved, w_down, v_down):
    rows, up_pre, gate_dot, up_dot, active, slope, curve, act_dot, hidden, hidden_dot = saved
    cot_rows = jnp.concatenate(cot_blocks, axis=1)
    grad_hid = jnp.einsum("erd,efd->efr", cot_rows, w_down, preferred_element_type=jnp.float32)
    hdot_early = jnp.einsum("erd,efd->efr", cot_rows, v_down, preferred_element_type=jnp.float32)
    down_early = jnp.einsum("efr,erd->efd", hidden_dot, cot_rows, preferred_element_type=jnp.float32)
    cdot_rows = jnp.concatenate(cdot_blocks, axis=1)
    grad_hdot = jnp.einsum("erd,efd->efr", cdot_rows, w_down, preferred_element_type=jnp.float32) + hdot_early
    hvp_down = down_early + jnp.einsum("efr,erd->efd", hidden, cdot_rows, preferred_element_type=jnp.float32)
    gate_term = (
        (grad_hdot * up_pre + grad_hid * up_dot) * slope + grad_hid * up_pre * curve * gate_dot
    ).astype(jnp.bfloat16)
    up_term = (grad_hdot * active + grad_hid * act_dot).astype(jnp.bfloat16)
    both_terms = jnp.stack([gate_term, up_term], axis=1)
    hvp_gate_up = jnp.einsum("ekfr,erd->ekfd", both_terms, rows, preferred_element_type=jnp.float32)
    return hvp_gate_up, hvp_down


def local(tokens, targets, router, picks, w_gate_up, w_down, v_gate_up, v_down):
    highest = lax.Precision.HIGHEST
    n_exp = lax.axis_size("expert")
    exp_dev = w_down.shape[0]
    onehot = picks.astype(jnp.bfloat16)
    gates = jax.nn.sigmoid(jnp.dot(tokens, router, preferred_element_type=jnp.float32))
    outgoing = jnp.einsum("tec,td->ecd", onehot, tokens, preferred_element_type=jnp.float32).astype(
        jnp.bfloat16
    )
    arrived = lax.all_to_all(outgoing, "expert", split_axis=0, concat_axis=0, tiled=True)
    row_blocks = tree_gather(regroup(arrived, exp_dev), 1)
    block_rows = row_blocks[0].shape[1]
    scale = 1.0 / math.sqrt(block_rows * len(row_blocks))
    groups = (row_blocks[:1], row_blocks[1:4], row_blocks[4:7], row_blocks[7:])
    parts, saved = [], []
    for blocks in groups:
        part, kept = forward_group(jnp.concatenate(blocks, axis=1), w_gate_up, w_down, v_gate_up, v_down)
        parts += [part[:, :, i * block_rows:(i + 1) * block_rows] for i in range(len(blocks))]
        saved.append(kept)
    own_out = tree_scatter_sum([part[0] for part in parts], 1)
    dot_parts, own_out = lax.optimization_barrier(([part[1] for part in parts], own_out))
    own_dot = tree_scatter_sum(dot_parts, 1)
    weighted = picks.astype(jnp.float32) * gates[:, :, None]
    ret_out = lax.all_to_all(
        regroup(own_out.astype(jnp.bfloat16), n_exp), "expert", split_axis=0, concat_axis=0, tiled=True
    )
    combined = jnp.einsum("tec,ecd->td", weighted, ret_out.astype(jnp.float32), precision=highest)
    mixed = combined.astype(jnp.bfloat16)
    resid = scale * (combined - targets.astype(jnp.float32))
    cot_send = jnp.einsum("tec,td->ecd", weighted, resid, precision=highest).astype(jnp.bfloat16)
    cot_got = lax.all_to_all(cot_send, "expert", split_axis=0, concat_axis=0, tiled=True)
    cot_blocks = tree_gather(regroup(cot_got, exp_dev), 1)
    dot_back, cot_got = lax.optimization_barrier((regroup(own_dot.astype(jnp.bfloat16), n_exp), cot_got))
    ret_dot = lax.all_to_all(dot_back, "expert", split_axis=0, concat_axis=0, tiled=True)
    combined_dot = jnp.einsum("tec,ecd->td", weighted, ret_dot.astype(jnp.float32), precision=highest)
    resid_dot = scale * combined_dot
    cdot_send = jnp.einsum("tec,td->ecd", weighted, resid_dot, precision=highest).astype(
        jnp.bfloat16
    )
    cdot_got = lax.all_to_all(cdot_send, "expert", split_axis=0, concat_axis=0, tiled=True)
    cdot_blocks = tree_gather(regroup(cdot_got, exp_dev), 1)
    hvp_gate_up, hvp_down = backward_group(cot_blocks[:1], cdot_blocks[:1], saved[0], w_down, v_down)
    for part, kept in zip((slice(1, 4), slice(4, 7), slice(7, 8)), saved[1:]):
        more_gate_up, more_down = backward_group(cot_blocks[part], cdot_blocks[part], kept, w_down, v_down)
        hvp_gate_up, hvp_down = (hvp_gate_up + more_gate_up, hvp_down + more_down)
    return (mixed, hvp_gate_up, hvp_down)


def solution(mesh):
    placed = (
        P(("expert", "dp"), None),
        P(("expert", "dp"), None),
        P(),
        P(("expert", "dp"), None, None),
        P("expert", None, "dp", None),
        P("expert", "dp", None),
        P("expert", None, "dp", None),
        P("expert", "dp", None),
    )
    return jax.shard_map(
        local,
        mesh=mesh,
        in_specs=placed,
        out_specs=(
            P(("expert", "dp"), None),
            P("expert", None, "dp", None),
            P("expert", "dp", None),
        ),
        check_vma=False,
    )
```

```python
import math

import jax
import jax.numpy as jnp
from jax import lax
from jax.sharding import PartitionSpec as P


def regroup(block, lead):
    count, total, width = block.shape
    parted = block.reshape(count, lead, total // lead, width)
    return jnp.swapaxes(parted, 0, 1).reshape(lead, count * total // lead, width)


def _perms(n_dp):
    nx = n_dp // 2
    idx = lambda a, b: 2 * (a % nx) + b
    partner = [(idx(a, b), idx(a, 1 - b)) for a in range(nx) for b in range(2)]
    xplus = [(idx(a, b), idx(a + 1, b)) for a in range(nx) for b in range(2)]
    xminus = [(idx(a, b), idx(a - 1, b)) for a in range(nx) for b in range(2)]
    return partner, xplus, xminus


def tree_gather(block, axis):
    partner, xplus, xminus = _perms(lax.axis_size("dp"))
    send = lambda v, perm: lax.ppermute(v, "dp", perm)
    half = block.shape[axis] // 2
    first = lambda v: lax.slice_in_dim(v, 0, half, axis=axis)
    second = lambda v: lax.slice_in_dim(v, half, v.shape[axis], axis=axis)
    Pb = send(block, partner)
    L = send(block, xplus)
    R = send(block, xminus)
    O = jnp.concatenate([send(first(L), xplus), send(second(R), xminus)], axis=axis)
    PL = send(Pb, xplus)
    PR = send(Pb, xminus)
    Q = send(O, partner)
    return [block, Pb, L, R, O, PL, PR, Q]


def tree_scatter_sum(acc, axis):
    partner, xplus, xminus = _perms(lax.axis_size("dp"))
    send = lambda v, perm: lax.ppermute(v.astype(jnp.bfloat16), "dp", perm).astype(jnp.float32)
    half = acc[0].shape[axis] // 2
    first = lambda v: lax.slice_in_dim(v, 0, half, axis=axis)
    second = lambda v: lax.slice_in_dim(v, half, v.shape[axis], axis=axis)
    a4 = acc[4] + send(acc[7], partner)
    a2 = acc[2] + jnp.concatenate([send(first(a4), xminus), jnp.zeros_like(second(a4))], axis=axis)
    a3 = acc[3] + jnp.concatenate([jnp.zeros_like(first(a4)), send(second(a4), xplus)], axis=axis)
    a1 = acc[1] + send(acc[5], xminus) + send(acc[6], xplus)
    return acc[0] + send(a1, partner) + send(a2, xminus) + send(a3, xplus)


def forward_group(rows, w_gate_up, w_down, v_gate_up, v_down):
    primal = jnp.einsum("ekfd,erd->ekfr", w_gate_up, rows, preferred_element_type=jnp.float32)
    tangent = jnp.einsum("ekfd,erd->ekfr", v_gate_up, rows, preferred_element_type=jnp.float32)
    gate_pre, up_pre = (primal[:, 0], primal[:, 1])
    gate_dot, up_dot = (tangent[:, 0], tangent[:, 1])
    sigma = jax.nn.sigmoid(gate_pre)
    active = gate_pre * sigma
    slope = sigma * (1.0 + gate_pre * (1.0 - sigma))
    curve = sigma * (1.0 - sigma) * (2.0 + gate_pre * (1.0 - 2.0 * sigma))
    act_dot = slope * gate_dot
    hidden = (active * up_pre).astype(jnp.bfloat16)
    hidden_dot = (act_dot * up_pre + active * up_dot).astype(jnp.bfloat16)
    part_out = jnp.einsum("efr,efd->erd", hidden, w_down, preferred_element_type=jnp.float32)
    saved = (rows, up_pre, gate_dot, up_dot, active, slope, curve, act_dot, hidden, hidden_dot)
    return part_out, saved


def tangent_part(hidden, hidden_dot, w_down, v_down):
    return jnp.einsum(
        "efr,efd->erd", hidden_dot, w_down, preferred_element_type=jnp.float32
    ) + jnp.einsum("efr,efd->erd", hidden, v_down, preferred_element_type=jnp.float32)


def backward_group(cot_blocks, cdot_blocks, saved, w_down, v_down):
    rows, up_pre, gate_dot, up_dot, active, slope, curve, act_dot, hidden, hidden_dot = saved
    cot_rows = jnp.concatenate(cot_blocks, axis=1)
    grad_hid = jnp.einsum("erd,efd->efr", cot_rows, w_down, preferred_element_type=jnp.float32)
    hdot_early = jnp.einsum("erd,efd->efr", cot_rows, v_down, preferred_element_type=jnp.float32)
    down_early = jnp.einsum("efr,erd->efd", hidden_dot, cot_rows, preferred_element_type=jnp.float32)
    cdot_rows = jnp.concatenate(cdot_blocks, axis=1)
    grad_hdot = jnp.einsum("erd,efd->efr", cdot_rows, w_down, preferred_element_type=jnp.float32) + hdot_early
    hvp_down = down_early + jnp.einsum("efr,erd->efd", hidden, cdot_rows, preferred_element_type=jnp.float32)
    gate_term = (
        (grad_hdot * up_pre + grad_hid * up_dot) * slope + grad_hid * up_pre * curve * gate_dot
    ).astype(jnp.bfloat16)
    up_term = (grad_hdot * active + grad_hid * act_dot).astype(jnp.bfloat16)
    both_terms = jnp.stack([gate_term, up_term], axis=1)
    hvp_gate_up = jnp.einsum("ekfr,erd->ekfd", both_terms, rows, preferred_element_type=jnp.float32)
    return hvp_gate_up, hvp_down


def local(tokens, targets, router, picks, w_gate_up, w_down, v_gate_up, v_down):
    highest = lax.Precision.HIGHEST
    n_exp = lax.axis_size("expert")
    exp_dev = w_down.shape[0]
    onehot = picks.astype(jnp.bfloat16)
    gates = jax.nn.sigmoid(jnp.dot(tokens, router, preferred_element_type=jnp.float32))
    outgoing = jnp.einsum("tec,td->ecd", onehot, tokens, preferred_element_type=jnp.float32).astype(
        jnp.bfloat16
    )
    arrived = lax.all_to_all(outgoing, "expert", split_axis=0, concat_axis=0, tiled=True)
    row_blocks = tree_gather(regroup(arrived, exp_dev), 1)
    block_rows = row_blocks[0].shape[1]
    scale = 1.0 / math.sqrt(block_rows * len(row_blocks))
    groups = (row_blocks[:4], row_blocks[4:7], row_blocks[7:])
    parts, saved = [], []
    for blocks in groups:
        part, kept = forward_group(jnp.concatenate(blocks, axis=1), w_gate_up, w_down, v_gate_up, v_down)
        parts += [part[:, i * block_rows:(i + 1) * block_rows] for i in range(len(blocks))]
        saved.append(kept)
    own_out = tree_scatter_sum(parts, 1)
    hiddens, own_out = lax.optimization_barrier(([(kept[8], kept[9]) for kept in saved], own_out))
    dot_parts = []
    for (hidden, hidden_dot), blocks in zip(hiddens, groups):
        part = tangent_part(hidden, hidden_dot, w_down, v_down)
        dot_parts += [part[:, i * block_rows:(i + 1) * block_rows] for i in range(len(blocks))]
    own_dot = tree_scatter_sum(dot_parts, 1)
    weighted = picks.astype(jnp.float32) * gates[:, :, None]
    ret_out = lax.all_to_all(
        regroup(own_out.astype(jnp.bfloat16), n_exp), "expert", split_axis=0, concat_axis=0, tiled=True
    )
    combined = jnp.einsum("tec,ecd->td", weighted, ret_out.astype(jnp.float32), precision=highest)
    mixed = combined.astype(jnp.bfloat16)
    resid = scale * (combined - targets.astype(jnp.float32))
    cot_send = jnp.einsum("tec,td->ecd", weighted, resid, precision=highest).astype(jnp.bfloat16)
    cot_got = lax.all_to_all(cot_send, "expert", split_axis=0, concat_axis=0, tiled=True)
    cot_blocks = tree_gather(regroup(cot_got, exp_dev), 1)
    dot_back, cot_got = lax.optimization_barrier((regroup(own_dot.astype(jnp.bfloat16), n_exp), cot_got))
    ret_dot = lax.all_to_all(dot_back, "expert", split_axis=0, concat_axis=0, tiled=True)
    combined_dot = jnp.einsum("tec,ecd->td", weighted, ret_dot.astype(jnp.float32), precision=highest)
    resid_dot = scale * combined_dot
    cdot_send = jnp.einsum("tec,td->ecd", weighted, resid_dot, precision=highest).astype(
        jnp.bfloat16
    )
    cdot_got = lax.all_to_all(cdot_send, "expert", split_axis=0, concat_axis=0, tiled=True)
    cdot_blocks = tree_gather(regroup(cdot_got, exp_dev), 1)
    hvp_gate_up, hvp_down = backward_group(cot_blocks[:4], cdot_blocks[:4], saved[0], w_down, v_down)
    for part, kept in zip((slice(4, 7), slice(7, 8)), saved[1:]):
        more_gate_up, more_down = backward_group(cot_blocks[part], cdot_blocks[part], kept, w_down, v_down)
        hvp_gate_up, hvp_down = (hvp_gate_up + more_gate_up, hvp_down + more_down)
    return (mixed, hvp_gate_up, hvp_down)


def solution(mesh):
    placed = (
        P(("expert", "dp"), None),
        P(("expert", "dp"), None),
        P(),
        P(("expert", "dp"), None, None),
        P("expert", None, "dp", None),
        P("expert", "dp", None),
        P("expert", None, "dp", None),
        P("expert", "dp", None),
    )
    return jax.shard_map(
        local,
        mesh=mesh,
        in_specs=placed,
        out_specs=(
            P(("expert", "dp"), None),
            P("expert", None, "dp", None),
            P("expert", "dp", None),
        ),
        check_vma=False,
    )
```

```python
import math

import jax
import jax.numpy as jnp
from jax import lax
from jax.sharding import PartitionSpec as P


def regroup(block, lead):
    count, total, width = block.shape
    parted = block.reshape(count, lead, total // lead, width)
    return jnp.swapaxes(parted, 0, 1).reshape(lead, count * total // lead, width)


def _perms(n_dp):
    nx = n_dp // 2
    idx = lambda a, b: 2 * (a % nx) + b
    partner = [(idx(a, b), idx(a, 1 - b)) for a in range(nx) for b in range(2)]
    xplus = [(idx(a, b), idx(a + 1, b)) for a in range(nx) for b in range(2)]
    xminus = [(idx(a, b), idx(a - 1, b)) for a in range(nx) for b in range(2)]
    return partner, xplus, xminus


def tree_gather(block, axis):
    partner, xplus, xminus = _perms(lax.axis_size("dp"))
    send = lambda v, perm: lax.ppermute(v, "dp", perm)
    half = block.shape[axis] // 2
    first = lambda v: lax.slice_in_dim(v, 0, half, axis=axis)
    second = lambda v: lax.slice_in_dim(v, half, v.shape[axis], axis=axis)
    Pb = send(block, partner)
    L = send(block, xplus)
    R = send(block, xminus)
    O = jnp.concatenate([send(first(L), xplus), send(second(R), xminus)], axis=axis)
    PL = send(Pb, xplus)
    PR = send(Pb, xminus)
    Q = send(O, partner)
    return [block, Pb, L, R, O, PL, PR, Q]


def tree_scatter_sum(acc, axis):
    partner, xplus, xminus = _perms(lax.axis_size("dp"))
    send = lambda v, perm: lax.ppermute(v.astype(jnp.bfloat16), "dp", perm).astype(jnp.float32)
    half = acc[0].shape[axis] // 2
    first = lambda v: lax.slice_in_dim(v, 0, half, axis=axis)
    second = lambda v: lax.slice_in_dim(v, half, v.shape[axis], axis=axis)
    a4 = acc[4] + send(acc[7], partner)
    a2 = acc[2] + jnp.concatenate([send(first(a4), xminus), jnp.zeros_like(second(a4))], axis=axis)
    a3 = acc[3] + jnp.concatenate([jnp.zeros_like(first(a4)), send(second(a4), xplus)], axis=axis)
    a1 = acc[1] + send(acc[5], xminus) + send(acc[6], xplus)
    return acc[0] + send(a1, partner) + send(a2, xminus) + send(a3, xplus)


def forward_group(rows, w_gate_up, w_down, v_gate_up, v_down):
    primal = jnp.einsum("ekfd,erd->ekfr", w_gate_up, rows, preferred_element_type=jnp.float32)
    tangent = jnp.einsum("ekfd,erd->ekfr", v_gate_up, rows, preferred_element_type=jnp.float32)
    gate_pre, up_pre = (primal[:, 0], primal[:, 1])
    gate_dot, up_dot = (tangent[:, 0], tangent[:, 1])
    sigma = jax.nn.sigmoid(gate_pre)
    active = gate_pre * sigma
    slope = sigma * (1.0 + gate_pre * (1.0 - sigma))
    curve = sigma * (1.0 - sigma) * (2.0 + gate_pre * (1.0 - 2.0 * sigma))
    act_dot = slope * gate_dot
    hidden = (active * up_pre).astype(jnp.bfloat16)
    hidden_dot = (act_dot * up_pre + active * up_dot).astype(jnp.bfloat16)
    part_out = jnp.einsum("efr,efd->erd", hidden, w_down, preferred_element_type=jnp.float32)
    saved = (rows, up_pre, gate_dot, up_dot, active, slope, curve, act_dot, hidden, hidden_dot)
    return part_out, saved


def tangent_part(hidden, hidden_dot, w_down, v_down):
    return jnp.einsum(
        "efr,efd->erd", hidden_dot, w_down, preferred_element_type=jnp.float32
    ) + jnp.einsum("efr,efd->erd", hidden, v_down, preferred_element_type=jnp.float32)


def backward_group(cot_blocks, cdot_blocks, saved, w_down, v_down):
    rows, up_pre, gate_dot, up_dot, active, slope, curve, act_dot, hidden, hidden_dot = saved
    cot_rows = jnp.concatenate(cot_blocks, axis=1)
    grad_hid = jnp.einsum("erd,efd->efr", cot_rows, w_down, preferred_element_type=jnp.float32)
    hdot_early = jnp.einsum("erd,efd->efr", cot_rows, v_down, preferred_element_type=jnp.float32)
    down_early = jnp.einsum("efr,erd->efd", hidden_dot, cot_rows, preferred_element_type=jnp.float32)
    cdot_rows = jnp.concatenate(cdot_blocks, axis=1)
    grad_hdot = jnp.einsum("erd,efd->efr", cdot_rows, w_down, preferred_element_type=jnp.float32) + hdot_early
    hvp_down = down_early + jnp.einsum("efr,erd->efd", hidden, cdot_rows, preferred_element_type=jnp.float32)
    gate_term = (
        (grad_hdot * up_pre + grad_hid * up_dot) * slope + grad_hid * up_pre * curve * gate_dot
    ).astype(jnp.bfloat16)
    up_term = (grad_hdot * active + grad_hid * act_dot).astype(jnp.bfloat16)
    both_terms = jnp.stack([gate_term, up_term], axis=1)
    hvp_gate_up = jnp.einsum("ekfr,erd->ekfd", both_terms, rows, preferred_element_type=jnp.float32)
    return hvp_gate_up, hvp_down


def local(tokens, targets, router, picks, w_gate_up, w_down, v_gate_up, v_down):
    highest = lax.Precision.HIGHEST
    n_exp = lax.axis_size("expert")
    exp_dev = w_down.shape[0]
    onehot = picks.astype(jnp.bfloat16)
    gates = jax.nn.sigmoid(jnp.dot(tokens, router, preferred_element_type=jnp.float32))
    outgoing = jnp.einsum("tec,td->ecd", onehot, tokens, preferred_element_type=jnp.float32).astype(
        jnp.bfloat16
    )
    arrived = lax.all_to_all(outgoing, "expert", split_axis=0, concat_axis=0, tiled=True)
    row_blocks = tree_gather(regroup(arrived, exp_dev), 1)
    block_rows = row_blocks[0].shape[1]
    scale = 1.0 / math.sqrt(block_rows * len(row_blocks))
    groups = (row_blocks[:4], row_blocks[4:7], row_blocks[7:])
    parts, saved = [], []
    for blocks in groups:
        part, kept = forward_group(jnp.concatenate(blocks, axis=1), w_gate_up, w_down, v_gate_up, v_down)
        parts += [part[:, i * block_rows:(i + 1) * block_rows] for i in range(len(blocks))]
        saved.append(kept)
    own_out = tree_scatter_sum(parts, 1)
    hiddens, own_out = lax.optimization_barrier(([(kept[8], kept[9]) for kept in saved], own_out))
    dot_parts = []
    for (hidden, hidden_dot), blocks in zip(hiddens, groups):
        part = tangent_part(hidden, hidden_dot, w_down, v_down)
        dot_parts += [part[:, i * block_rows:(i + 1) * block_rows] for i in range(len(blocks))]
    own_dot = tree_scatter_sum(dot_parts, 1)
    weighted = picks.astype(jnp.float32) * gates[:, :, None]
    ret_out = lax.all_to_all(
        regroup(own_out.astype(jnp.bfloat16), n_exp), "expert", split_axis=0, concat_axis=0, tiled=True
    )
    combined = jnp.einsum("tec,ecd->td", weighted, ret_out.astype(jnp.float32), precision=highest)
    mixed = combined.astype(jnp.bfloat16)
    resid = scale * (combined - targets.astype(jnp.float32))
    cot_send = jnp.einsum("tec,td->ecd", weighted, resid, precision=highest).astype(jnp.bfloat16)
    cot_got = lax.all_to_all(cot_send, "expert", split_axis=0, concat_axis=0, tiled=True)
    cot_blocks = tree_gather(regroup(cot_got, exp_dev), 1)
    dot_back, cot_got = lax.optimization_barrier((regroup(own_dot.astype(jnp.bfloat16), n_exp), cot_got))
    ret_dot = lax.all_to_all(dot_back, "expert", split_axis=0, concat_axis=0, tiled=True)
    combined_dot = jnp.einsum("tec,ecd->td", weighted, ret_dot.astype(jnp.float32), precision=highest)
    resid_dot = scale * combined_dot
    cdot_send = jnp.einsum("tec,td->ecd", weighted, resid_dot, precision=highest).astype(
        jnp.bfloat16
    )
    cdot_send, cot_blocks = lax.optimization_barrier((cdot_send, cot_blocks))
    cdot_got = lax.all_to_all(cdot_send, "expert", split_axis=0, concat_axis=0, tiled=True)
    cdot_blocks = tree_gather(regroup(cdot_got, exp_dev), 1)
    hvp_gate_up, hvp_down = backward_group(cot_blocks[:4], cdot_blocks[:4], saved[0], w_down, v_down)
    for part, kept in zip((slice(4, 7), slice(7, 8)), saved[1:]):
        more_gate_up, more_down = backward_group(cot_blocks[part], cdot_blocks[part], kept, w_down, v_down)
        hvp_gate_up, hvp_down = (hvp_gate_up + more_gate_up, hvp_down + more_down)
    return (mixed, hvp_gate_up, hvp_down)


def solution(mesh):
    placed = (
        P(("expert", "dp"), None),
        P(("expert", "dp"), None),
        P(),
        P(("expert", "dp"), None, None),
        P("expert", None, "dp", None),
        P("expert", "dp", None),
        P("expert", None, "dp", None),
        P("expert", "dp", None),
    )
    return jax.shard_map(
        local,
        mesh=mesh,
        in_specs=placed,
        out_specs=(
            P(("expert", "dp"), None),
            P("expert", None, "dp", None),
            P("expert", "dp", None),
        ),
        check_vma=False,
    )
```
